128 devices in a mesh: req: 8 (over z, core), shard: 16 (over x, y).
Axes of the slice: x: 4, y: 4, z: 4, core: 2. Of those that a mesh axis runs over, the one named last changes fastest.
Arguments:
- hidden_states: bfloat16 [16384, 1536], P(('req', 'shard')), may hold values from -6 to 6
- attn_gain: float32 [1536], replicated, may hold values from 0.5 to 1.5
- w_qkv: bfloat16 [1536, 2560], replicated, may hold values from -0.15625 to 0.15625
- w_out: bfloat16 [1536, 1536], replicated, may hold values from -0.15625 to 0.15625
- kv_cache: bfloat16 [8, 4096, 1024], P('req', 'shard'), may hold values from -80 to 80, as said below
- cached_len: int32 [8], P('req'), may hold values from 128 to 4096, as said below
- ffn_gain: float32 [1536], replicated, may hold values from 0.5 to 1.5
- w_router: bfloat16 [1536, 40], replicated, may hold values from -0.15625 to 0.15625
- expert_ids: int32 [16384, 8], P(('req', 'shard')), may hold values from 0 to 39, all different within a row; in each aligned block of 128 rows (0 to 127, 128 to 255, ...) at most 32 rows name the same one
- w_gate: bfloat16 [40, 512, 1536], P('req', 'shard'), may hold values from -0.15625 to 0.15625
- w_up: bfloat16 [40, 512, 1536], P('req', 'shard'), may hold values from -0.15625 to 0.15625
- w_down: bfloat16 [40, 512, 1536], P('req', 'shard'), may hold values from -0.25 to 0.25
Outputs:
- layer_out: bfloat16 [16384, 1536], P(('req', 'shard'))
The draws below stay inside these ranges and needn't reach their ends.
Inputs may be any that keep to these rules, and one draw needn't show every extreme that they name: `cached_len`: each request's length is drawn either between 128 and 512 or between 3072 and 4096; some request has exactly 4096. `expert_ids`: among the 128 rows of one device no expert is named by more than 32 rows. `kv_cache`: cached keys and values, already rotated.
All inputs are finite; a program needn't handle non-finite values.
Results may differ from the reference program's by a relative error of at most 0.025.
Values may be sent and summed in bfloat16 or wider, within the bound.
No kernel may reach another device: no remote copies, remote signals or barrier semaphores. Data moves between devices by JAX's collectives and lax.ppermute only.
A program may use at most 192 MiB of HBM per device.

```python
import math
import jax
import jax.numpy as jnp
import numpy as np
from jax import lax

D = 1536
HEADS = 24
KVH = 8
HD = 64
EFF = 512
TOP = 8
TOK_DEV = 128
REQS = 8
NEWTOK = 2048
CACHE = 4096
TOKENS = 16384
EXPERTS = 40
CAP = 32
N_REQ = 8
N_SHARD = 16


def draw_cached_len(key, part):
    mode_key, short_key, long_key, pick_key = jax.random.split(jax.random.fold_in(key, 11), 4)
    mode_bits = jax.random.randint(mode_key, (REQS,), 0, 2)
    short_len = jax.random.randint(short_key, (REQS,), CACHE // 32, CACHE // 8 + 1)
    long_len = jax.random.randint(long_key, (REQS,), 3 * CACHE // 4, CACHE + 1)
    lengths = jnp.where(mode_bits == 1, long_len, short_len)
    chosen = jax.random.randint(pick_key, (), 0, REQS)
    lengths = jnp.where(jnp.arange(REQS) == chosen, CACHE, lengths)
    return lengths.astype(jnp.int32)


def draw_kv_cache(key, part):
    base_key = jax.random.fold_in(jax.random.fold_in(key, 23), 0)
    columns = 2 * KVH * HD
    values = jax.random.normal(base_key, (REQS, CACHE, columns), jnp.float32)
    return values.astype(jnp.bfloat16)


def steps_of(own_key, dims, pieces, smallest, high):
    level, own = 1.0, jax.random.fold_in(own_key, 6)
    for axis_at, shards_of in pieces:
        steps = jnp.exp(jax.random.uniform(jax.random.fold_in(own, axis_at), (shards_of,), jnp.float32, smallest / len(pieces), high / len(pieces)))
        level = level * jnp.repeat(steps, dims[axis_at] // shards_of).reshape([-1 if axis == axis_at else 1 for axis in range(len(dims))])
    return level


def deal_out(own_key, own, number, rows, count, top, most, lean):
    sequence = jax.random.permutation(own_key, count)
    crowded, ordinary = portions_of(count, rows * top, most, lean, True), portions_of(count, rows * top, most, lean, False)
    places = jnp.arange(count)

    def named(sizes, rotation):
        used = int((sizes > 0).sum())
        fixed = max(1, used // 4)
        moved = fixed + (places - fixed + rotation * (used - fixed)) % max(1, count - fixed)
        return jnp.zeros((count,), jnp.int32).at[sequence[jnp.where(places < fixed, places, moved)]].set(jnp.asarray(sizes, jnp.int32))

    sizes = jnp.where(number % 4 == 0, named(crowded, number // 4), named(ordinary, number - number // 4 - 1))
    mixed = jax.random.permutation(jax.random.fold_in(own, 3), count)
    donor, receiver = mixed[0:count // 2 * 2:2], mixed[1:count // 2 * 2:2]
    room = jnp.minimum(sizes[donor] - 1, most - sizes[receiver]) // 2
    room = jnp.where((donor == sequence[0]) | (receiver == sequence[0]) | (sizes[receiver] == 0), 0, jnp.maximum(room, 0))
    moved = jax.random.randint(jax.random.fold_in(own, 4), (count // 2,), 0, 1 << 20) % (room + 1)
    sizes = sizes.at[donor].add(-moved).at[receiver].add(moved)
    members = jnp.searchsorted(jnp.cumsum(sizes), jnp.arange(rows * top), side="right").astype(jnp.int32)
    grid = members.reshape(top, rows).T
    grid = grid[jax.random.permutation(jax.random.fold_in(own, 1), rows)]
    rotation = jax.random.randint(jax.random.fold_in(own, 2), (rows, 1), 0, top)
    return jnp.take_along_axis(grid, (jnp.arange(top)[None, :] + rotation) % top, axis=1)


def portions_of(number_of, total, limit, lean, full):
    loads = [(1 << 20) // math.isqrt(standing ** lean) + 1 for standing in range(1, number_of + 1)]
    largest = limit if full else min(limit, max(-(-total // number_of), total * loads[0] // sum(loads)))
    least = 1 if total - largest >= number_of - 1 else 0
    given, surplus = [largest] + [least] * (number_of - 1), total - largest - least * (number_of - 1)
    while surplus > 0:
        free = [i for i in range(1, number_of) if given[i] < largest] or [i for i in range(1, number_of) if given[i] < limit]
        pool, budget = sum([loads[i] for i in free]), surplus
        for i in free:
            extra = min(limit - given[i], max(1, budget * loads[i] // pool), surplus)
            given[i] = given[i] + extra
            surplus = surplus - extra
    return np.array(given)


def scatter_about(rng, extent, width, limit, cuts=(), kind=jnp.bfloat16):
    level = steps_of(rng, extent, cuts, -0.22, 0.18) if cuts else 1.0
    array = jax.random.normal(rng, extent, jnp.float32) * width * level
    return jnp.minimum(jnp.maximum(array, -limit), limit).astype(kind)


def setup_inputs(seed: int = 0) -> dict:
    arg_keys = jax.random.split(jax.random.key(seed), 13)
    hidden_states = scatter_about(arg_keys[0], (TOKENS, D), 1.0, 6.0, ((0, 128),))
    attn_gain = jnp.clip(1.0 + 0.1 * jax.random.normal(arg_keys[1], (D,), jnp.float32), 0.5, 1.5)
    w_qkv = scatter_about(arg_keys[2], (D, (HEADS + 2 * KVH) * HD), D ** -0.5, 0.15625)
    w_out = scatter_about(arg_keys[3], (HEADS * HD, D), (HEADS * HD) ** -0.5, 0.15625)
    kv_cache = draw_kv_cache(jax.random.fold_in(arg_keys[12], 71), 0)
    cached_len = draw_cached_len(jax.random.fold_in(arg_keys[12], 71), 0)
    ffn_gain = jnp.clip(1.0 + 0.1 * jax.random.normal(arg_keys[6], (D,), jnp.float32), 0.5, 1.5)
    w_router = scatter_about(arg_keys[7], (D, EXPERTS), D ** -0.5, 0.15625)
    expert_ids_keys = jax.random.split(jax.random.fold_in(arg_keys[8], 1), TOKENS // TOK_DEV)
    expert_ids_turns = jax.random.permutation(jax.random.fold_in(arg_keys[8], 3), TOKENS // TOK_DEV)
    expert_ids = jax.vmap(lambda own, number: deal_out(jax.random.fold_in(arg_keys[8], 2), own, number, TOK_DEV, EXPERTS, TOP, CAP, 2))(expert_ids_keys, expert_ids_turns).reshape((TOKENS, TOP))
    w_gate = scatter_about(arg_keys[9], (EXPERTS, EFF, D), D ** -0.5, 0.15625, ((0, 8), (1, 16)))
    w_up = scatter_about(arg_keys[10], (EXPERTS, EFF, D), D ** -0.5, 0.15625, ((0, 8), (1, 16)))
    w_down = scatter_about(arg_keys[11], (EXPERTS, EFF, D), EFF ** -0.5, 0.25, ((0, 8), (1, 16)))
    return {"hidden_states": hidden_states, "attn_gain": attn_gain, "w_qkv": w_qkv, "w_out": w_out, "kv_cache": kv_cache, "cached_len": cached_len, "ffn_gain": ffn_gain, "w_router": w_router, "expert_ids": expert_ids, "w_gate": w_gate, "w_up": w_up, "w_down": w_down}


EPSILON = 1e-05
NEG_FILL = -1e+30
FAR_LIMIT = 1 << 30

def rms_scale(values, gain):
    floats = values.astype(jnp.float32)
    inverse = lax.rsqrt(lax.optimization_barrier(jnp.mean(floats * floats, axis=-1, keepdims=True)) + EPSILON)
    return (floats * inverse * gain).astype(jnp.bfloat16)

def rotate(values, positions):
    half_dim = values.shape[-1] // 2
    freqs = jnp.power(10000.0, -jnp.arange(half_dim, dtype=jnp.float32) / half_dim).astype(jnp.float32)
    angles = positions.astype(jnp.float32)[:, None] * freqs[None, :]
    cosine = jnp.cos(angles)[:, None, :]
    sine = jnp.sin(angles)[:, None, :]
    first = values[..., :half_dim]
    second = values[..., half_dim:]
    return jnp.concatenate([first * cosine - second * sine, second * cosine + first * sine], axis=-1)

def attend_request(query_rows, key_rows, value_rows, cache_rows, length):
    groups = HEADS // KVH
    keys = jnp.concatenate([cache_rows[:, :KVH * HD], key_rows], axis=0).reshape(CACHE + NEWTOK, KVH, HD)
    values = jnp.concatenate([cache_rows[:, KVH * HD:], value_rows], axis=0).reshape(CACHE + NEWTOK, KVH, HD)
    key_pos = jnp.concatenate([jnp.arange(CACHE, dtype=jnp.int32), length + jnp.arange(NEWTOK, dtype=jnp.int32)])
    key_lim = jnp.concatenate([jnp.full((CACHE,), length, jnp.int32), jnp.full((NEWTOK,), FAR_LIMIT, jnp.int32)])
    key_float = keys.astype(jnp.float32)
    block_rows = math.gcd(NEWTOK, 256)
    count = NEWTOK // block_rows
    query_blocks = query_rows.reshape(count, block_rows, KVH, groups, HD)
    pos_blocks = (length + jnp.arange(NEWTOK, dtype=jnp.int32)).reshape(count, block_rows)

    def one_block(item):
        query_block, query_pos = item
        scores = jnp.einsum('tgqd,rgd->tgqr', query_block.astype(jnp.float32), key_float, precision=lax.Precision.HIGHEST) * HD ** (-0.5)
        allowed = (key_pos[None, :] <= query_pos[:, None]) & (key_pos < key_lim)[None, :]
        allowed = allowed[:, None, None, :]
        top = lax.optimization_barrier(jnp.max(jnp.where(allowed, scores, NEG_FILL), axis=-1, keepdims=True))
        weights = jnp.where(allowed, jnp.exp(scores - top), 0.0)
        total = lax.optimization_barrier(jnp.sum(weights, axis=-1))
        summed = jnp.einsum('tgqr,rgd->tgqd', weights.astype(jnp.bfloat16), values, preferred_element_type=jnp.float32)
        return (summed / total[..., None]).astype(jnp.bfloat16)
    result = lax.map(one_block, (query_blocks, pos_blocks))
    return result.reshape(NEWTOK, HEADS * HD)

def reference(hidden_states, attn_gain, w_qkv, w_out, kv_cache, cached_len, ffn_gain, w_router, expert_ids, w_gate, w_up, w_down):
    groups = HEADS // KVH
    normed = rms_scale(hidden_states, attn_gain)
    qkv = jnp.dot(normed, w_qkv, preferred_element_type=jnp.float32)
    positions = (cached_len[:, None] + jnp.arange(NEWTOK, dtype=jnp.int32)[None, :]).reshape(-1).astype(jnp.int32)
    queries = rotate(qkv[:, :HEADS * HD].reshape(TOKENS, HEADS, HD), positions).astype(jnp.bfloat16)
    new_keys = rotate(qkv[:, HEADS * HD:(HEADS + KVH) * HD].reshape(TOKENS, KVH, HD), positions).astype(jnp.bfloat16)
    new_values = qkv[:, (HEADS + KVH) * HD:].astype(jnp.bfloat16)
    query_req = queries.reshape(REQS, NEWTOK, KVH, groups, HD)
    key_req = new_keys.reshape(REQS, NEWTOK, KVH * HD)
    value_req = new_values.reshape(REQS, NEWTOK, KVH * HD)

    def per_request(item):
        return attend_request(item[0], item[1], item[2], item[3], item[4])
    attended = lax.map(per_request, (query_req, key_req, value_req, kv_cache, cached_len)).reshape(TOKENS, HEADS * HD)
    mid = (hidden_states.astype(jnp.float32) + jnp.dot(attended, w_out, preferred_element_type=jnp.float32)).astype(jnp.bfloat16)
    normed2 = rms_scale(mid, ffn_gain)
    logits = jnp.dot(normed2, w_router, preferred_element_type=jnp.float32)
    chosen = jnp.take_along_axis(logits, expert_ids, axis=1)
    gates = jax.nn.softmax(chosen, axis=-1)
    flat_ids = expert_ids.reshape(-1).astype(jnp.int32)
    order = jnp.argsort(flat_ids, stable=True).astype(jnp.int32)
    tok_sorted = (order // TOP).astype(jnp.int32)
    gate_sorted = gates.reshape(-1)[order]
    counts = jax.ops.segment_sum(jnp.ones_like(flat_ids), flat_ids, num_segments=EXPERTS).astype(jnp.int32)
    starts = (jnp.cumsum(counts) - counts).astype(jnp.int32)
    most = N_REQ * N_SHARD * CAP
    tok_pad = jnp.concatenate([tok_sorted, jnp.zeros((most,), jnp.int32)])
    gate_pad = jnp.concatenate([gate_sorted, jnp.zeros((most,), jnp.float32)])

    def expert_step(total, expert):
        begin = starts[expert]
        rows = lax.dynamic_slice(tok_pad, (begin,), (most,))
        weights = lax.dynamic_slice(gate_pad, (begin,), (most,))
        valid = jnp.arange(most, dtype=jnp.int32) < counts[expert]
        inputs = normed2[rows]
        gate = jnp.dot(inputs, w_gate[expert].T, preferred_element_type=jnp.float32)
        upper = jnp.dot(inputs, w_up[expert].T, preferred_element_type=jnp.float32)
        inner = (jax.nn.silu(gate) * upper).astype(jnp.bfloat16)
        output = jnp.dot(inner, w_down[expert], preferred_element_type=jnp.float32).astype(jnp.bfloat16)
        term = jnp.where(valid[:, None], weights[:, None] * output.astype(jnp.float32), 0.0)
        return (total.at[rows].add(term), None)
    mixture, _ = lax.scan(expert_step, jnp.zeros((TOKENS, D), jnp.float32), jnp.arange(EXPERTS, dtype=jnp.int32))
    return (mid.astype(jnp.float32) + mixture).astype(jnp.bfloat16)
```

```python
import math

import jax
import jax.numpy as jnp
from jax import lax
from jax.sharding import PartitionSpec as P

D = 1536
HEADS = 24
KVH = 8
HD = 64
TOP = 8


EPSILON = 1e-05
NEG_FILL = -1e30
FAR_LIMIT = 1 << 30


def rms_scale(values, gain):
    floats = values.astype(jnp.float32)
    inverse = lax.rsqrt(jnp.mean(floats * floats, axis=-1, keepdims=True) + EPSILON)
    return (floats * inverse * gain).astype(jnp.bfloat16)


def rotate(values, positions):
    half_dim = values.shape[-1] // 2
    freqs = jnp.power(10000.0, -jnp.arange(half_dim, dtype=jnp.float32) / half_dim)
    angles = positions.astype(jnp.float32)[:, None] * freqs[None, :]
    cosine = jnp.cos(angles)[:, None, :]
    sine = jnp.sin(angles)[:, None, :]
    first = values[..., :half_dim]
    second = values[..., half_dim:]
    return jnp.concatenate(
        [first * cosine - second * sine, second * cosine + first * sine], axis=-1
    )


def empty_state(rows):
    groups = HEADS // KVH
    return (
        jnp.full((rows, KVH, groups), NEG_FILL, jnp.float32),
        jnp.zeros((rows, KVH, groups), jnp.float32),
        jnp.zeros((rows, KVH, groups, HD), jnp.float32),
    )


def attend_block(state, queries, query_pos, block, key_pos, key_limit):
    max_run, total, accum = state
    rows = block.shape[0]
    keys = block[:, : KVH * HD].reshape(rows, KVH, HD)
    values = block[:, KVH * HD :].reshape(rows, KVH, HD)
    scores = jnp.einsum(
        "tgqd,rgd->tgqr", queries, keys, preferred_element_type=jnp.float32
    ) * HD ** (-0.5)
    allowed = (key_pos[None, :] <= query_pos[:, None]) & (key_pos < key_limit)[None, :]
    allowed = allowed[:, None, None, :]
    block_max = jnp.max(jnp.where(allowed, scores, NEG_FILL), axis=-1)
    new_max = jnp.maximum(max_run, block_max)
    weights = jnp.where(allowed, jnp.exp(scores - new_max[..., None]), 0.0)
    factor = jnp.exp(max_run - new_max)
    total = total * factor + jnp.sum(weights, axis=-1)
    accum = accum * factor[..., None] + jnp.einsum(
        "tgqr,rgd->tgqd", weights.astype(jnp.bfloat16), values, preferred_element_type=jnp.float32
    )
    return (new_max, total, accum)


def fold_rows(state, queries, query_pos, piece, key_pos, key_limit):
    rows = piece.shape[0]
    step_rows = math.gcd(rows, 512)
    count = rows // step_rows
    blocks = piece.reshape(count, step_rows, piece.shape[1])
    positions = key_pos.reshape(count, step_rows)

    def advance(carry, item):
        return (attend_block(carry, queries, query_pos, item[0], item[1], key_limit), None)

    state, _ = lax.scan(advance, state, (blocks, positions))
    return state


def local(
    hidden_states,
    attn_gain,
    w_qkv,
    w_out,
    kv_cache,
    cached_len,
    ffn_gain,
    w_router,
    expert_ids,
    w_gate,
    w_up,
    w_down,
):
    groups = HEADS // KVH
    tok_rows = hidden_states.shape[0]
    shard_pos = lax.axis_index("shard")
    length = cached_len[0]
    normed = rms_scale(hidden_states, attn_gain)
    qkv = jnp.dot(normed, w_qkv, preferred_element_type=jnp.float32)
    positions = length + shard_pos * tok_rows + jnp.arange(tok_rows, dtype=jnp.int32)
    queries = rotate(qkv[:, : HEADS * HD].reshape(tok_rows, HEADS, HD), positions).astype(
        jnp.bfloat16
    )
    new_keys = rotate(
        qkv[:, HEADS * HD : (HEADS + KVH) * HD].reshape(tok_rows, KVH, HD), positions
    ).astype(jnp.bfloat16)
    new_values = qkv[:, (HEADS + KVH) * HD :].astype(jnp.bfloat16)
    new_kv = jnp.concatenate([new_keys.reshape(tok_rows, KVH * HD), new_values], axis=1)
    cache_local = kv_cache[0]
    query_heads = queries.reshape(tok_rows, KVH, groups, HD)
    piece = lax.all_gather(cache_local, "shard", axis=0, tiled=True)
    key_pos = jnp.arange(piece.shape[0], dtype=jnp.int32)
    state = fold_rows(empty_state(tok_rows), query_heads, positions, piece, key_pos, length)
    piece = lax.all_gather(new_kv, "shard", axis=0, tiled=True)
    key_pos = length + jnp.arange(piece.shape[0], dtype=jnp.int32)
    max_run, total, accum = fold_rows(state, query_heads, positions, piece, key_pos, FAR_LIMIT)
    attended = (accum / total[..., None]).astype(jnp.bfloat16)
    attended = attended.reshape(tok_rows, HEADS * HD)
    mid = (
        hidden_states.astype(jnp.float32)
        + jnp.dot(attended, w_out, preferred_element_type=jnp.float32)
    ).astype(jnp.bfloat16)
    normed2 = rms_scale(mid, ffn_gain)
    group_count = lax.axis_size("req")
    local_experts = w_gate.shape[0]
    expert_count = local_experts * group_count
    capacity = min(tok_rows, 5 * tok_rows * TOP // (4 * expert_count))
    logits = jnp.dot(normed2, w_router, preferred_element_type=jnp.float32)
    picked = expert_ids[:, :, None] == jnp.arange(expert_count, dtype=jnp.int32)[None, None, :]
    chosen = jnp.sum(jnp.where(picked, logits[:, None, :], 0.0), axis=-1)
    gates = jax.nn.softmax(chosen, axis=-1)
    flat_hot = picked.reshape(tok_rows * TOP, expert_count).astype(jnp.int32)
    ranks = jnp.cumsum(flat_hot, axis=0) - flat_hot
    slot_rank = jnp.sum(ranks * flat_hot, axis=-1)
    slots = expert_ids.reshape(-1) * capacity + slot_rank
    slot_table = (
        slots.reshape(tok_rows, TOP)[:, :, None]
        == jnp.arange(expert_count * capacity, dtype=jnp.int32)[None, None, :]
    )
    placing = jnp.any(slot_table, axis=1).astype(jnp.bfloat16)
    outgoing = jnp.einsum("ts,td->sd", placing, normed2, preferred_element_type=jnp.float32).astype(
        jnp.bfloat16
    )
    outgoing = outgoing.reshape(group_count, local_experts, capacity, D)
    arrived = lax.all_to_all(outgoing, "req", split_axis=0, concat_axis=0, tiled=True)
    weights = jnp.concatenate([w_gate, w_up, w_down], axis=-1)
    weights = lax.all_gather(weights, "shard", axis=1, tiled=True)
    gate_piece = weights[..., :D]
    up_piece = weights[..., D : 2 * D]
    down_piece = weights[..., 2 * D :]
    gate = jnp.einsum("sjcd,jhd->sjch", arrived, gate_piece, preferred_element_type=jnp.float32)
    upper = jnp.einsum("sjcd,jhd->sjch", arrived, up_piece, preferred_element_type=jnp.float32)
    inner = (jax.nn.silu(gate) * upper).astype(jnp.bfloat16)
    summed = jnp.einsum("sjch,jhd->sjcd", inner, down_piece, preferred_element_type=jnp.float32)
    returned = lax.all_to_all(
        summed.astype(jnp.bfloat16), "req", split_axis=0, concat_axis=0, tiled=True
    )
    returned = returned.reshape(expert_count * capacity, D)
    expert_rows = returned[slots].reshape(tok_rows, TOP, D)
    mixture = jnp.sum(gates[:, :, None] * expert_rows.astype(jnp.float32), axis=1)
    return (mid.astype(jnp.float32) + mixture).astype(jnp.bfloat16)


def solution(mesh):
    return jax.shard_map(
        local,
        mesh=mesh,
        in_specs=(
            P(("req", "shard"), None),
            P(),
            P(),
            P(),
            P("req", "shard", None),
            P("req"),
            P(),
            P(),
            P(("req", "shard"), None),
            P("req", "shard", None),
            P("req", "shard", None),
            P("req", "shard", None),
        ),
        out_specs=P(("req", "shard"), None),
        check_vma=False,
    )
```

```python
import functools
import math

import jax
import jax.numpy as jnp
from jax import lax
from jax.experimental import pallas as pl
from jax.experimental.pallas import tpu as pltpu
from jax.sharding import PartitionSpec as P

D = 1536
HEADS = 24
KVH = 8
HD = 64
TOP = 8


EPSILON = 1e-05
NEG_FILL = -1e30
FAR_LIMIT = 1 << 30
BLK = 512
NEG = NEG_FILL

def attn_kernel(meta_ref, q_ref, cache_ref, new_ref, o_ref, m_sc, l_sc, acc_sc, *, n_cache, rows):
    i = pl.program_id(0)
    length = meta_ref[0]
    qbase = meta_ref[1]

    @pl.when(i == 0)
    def _():
        m_sc[...] = jnp.full(m_sc.shape, NEG, jnp.float32)
        l_sc[...] = jnp.zeros(l_sc.shape, jnp.float32)
        acc_sc[...] = jnp.zeros(acc_sc.shape, jnp.float32)

    def step(kv_ref, allowed):
        for g in range(KVH):
            q = q_ref[g]
            k = kv_ref[:, g * HD:(g + 1) * HD]
            v = kv_ref[:, KVH * HD + g * HD:KVH * HD + (g + 1) * HD]
            s = lax.dot_general(q, k, (((1,), (1,)), ((), ())), preferred_element_type=jnp.float32) * (HD ** -0.5)
            s = jnp.where(allowed, s, NEG)
            m_prev = m_sc[g]
            m_new = jnp.maximum(m_prev, jnp.max(s, axis=-1, keepdims=True))
            p = jnp.where(allowed, jnp.exp(s - m_new), 0.0)
            factor = jnp.exp(m_prev - m_new)
            l_sc[g] = l_sc[g] * factor + jnp.sum(p, axis=-1, keepdims=True)
            acc_sc[g] = acc_sc[g] * factor + jnp.dot(p.astype(jnp.bfloat16), v, preferred_element_type=jnp.float32)
            m_sc[g] = m_new

    @pl.when((i < n_cache) & (i * BLK < length))
    def _():
        key = i * BLK + lax.broadcasted_iota(jnp.int32, (rows, BLK), 1)
        step(cache_ref, key < length)

    j = i - n_cache
    @pl.when((i >= n_cache) & (j * BLK <= qbase + (rows // (HEADS // KVH)) - 1))
    def _():
        key = j * BLK + lax.broadcasted_iota(jnp.int32, (rows, BLK), 1)
        qpos = qbase + lax.broadcasted_iota(jnp.int32, (rows, BLK), 0) % (rows // (HEADS // KVH))
        step(new_ref, key <= qpos)

    @pl.when(i == pl.num_programs(0) - 1)
    def _():
        for g in range(KVH):
            o_ref[g] = (acc_sc[g] / l_sc[g]).astype(o_ref.dtype)

def attention(queries, cache, new_kv, length, qbase):
    rows = queries.shape[1]
    n_cache = cache.shape[0] // BLK
    n_new = new_kv.shape[0] // BLK
    meta = jnp.stack([length, qbase]).astype(jnp.int32)
    kern = functools.partial(attn_kernel, n_cache=n_cache, rows=rows)
    return pl.pallas_call(
        kern,
        out_shape=jax.ShapeDtypeStruct((KVH, rows, HD), jnp.bfloat16),
        grid_spec=pltpu.PrefetchScalarGridSpec(
            num_scalar_prefetch=1,
            grid=(n_cache + n_new,),
            in_specs=[
                pl.BlockSpec((KVH, rows, HD), lambda i, m: (0, 0, 0)),
                pl.BlockSpec((BLK, 2 * KVH * HD), lambda i, m: (jnp.minimum(i, n_cache - 1), 0)),
                pl.BlockSpec((BLK, 2 * KVH * HD), lambda i, m: (jnp.maximum(i - n_cache, 0), 0)),
            ],
            out_specs=pl.BlockSpec((KVH, rows, HD), lambda i, m: (0, 0, 0)),
            scratch_shapes=[
                pltpu.VMEM((KVH, rows, 1), jnp.float32),
                pltpu.VMEM((KVH, rows, 1), jnp.float32),
                pltpu.VMEM((KVH, rows, HD), jnp.float32),
            ],
        ),
        compiler_params=pltpu.CompilerParams(dimension_semantics=("arbitrary",)),
    )(meta, queries, cache, new_kv)


def rms_scale(values, gain):
    floats = values.astype(jnp.float32)
    inverse = lax.rsqrt(jnp.mean(floats * floats, axis=-1, keepdims=True) + EPSILON)
    return (floats * inverse * gain).astype(jnp.bfloat16)


def rotate(values, positions):
    half_dim = values.shape[-1] // 2
    freqs = jnp.power(10000.0, -jnp.arange(half_dim, dtype=jnp.float32) / half_dim)
    angles = positions.astype(jnp.float32)[:, None] * freqs[None, :]
    cosine = jnp.cos(angles)[:, None, :]
    sine = jnp.sin(angles)[:, None, :]
    first = values[..., :half_dim]
    second = values[..., half_dim:]
    return jnp.concatenate(
        [first * cosine - second * sine, second * cosine + first * sine], axis=-1
    )


def local(
    hidden_states,
    attn_gain,
    w_qkv,
    w_out,
    kv_cache,
    cached_len,
    ffn_gain,
    w_router,
    expert_ids,
    w_gate,
    w_up,
    w_down,
):
    groups = HEADS // KVH
    tok_rows = hidden_states.shape[0]
    shard_pos = lax.axis_index("shard")
    length = cached_len[0]
    normed = rms_scale(hidden_states, attn_gain)
    qkv = jnp.dot(normed, w_qkv, preferred_element_type=jnp.float32)
    positions = length + shard_pos * tok_rows + jnp.arange(tok_rows, dtype=jnp.int32)
    queries = rotate(qkv[:, : HEADS * HD].reshape(tok_rows, HEADS, HD), positions).astype(
        jnp.bfloat16
    )
    new_keys = rotate(
        qkv[:, HEADS * HD : (HEADS + KVH) * HD].reshape(tok_rows, KVH, HD), positions
    ).astype(jnp.bfloat16)
    new_values = qkv[:, (HEADS + KVH) * HD :].astype(jnp.bfloat16)
    new_kv = jnp.concatenate([new_keys.reshape(tok_rows, KVH * HD), new_values], axis=1)
    cache = lax.all_gather(kv_cache[0], "shard", axis=0, tiled=True)
    fresh = lax.all_gather(new_kv, "shard", axis=0, tiled=True)
    query_rows = queries.reshape(tok_rows, KVH, groups, HD).transpose(1, 2, 0, 3)
    query_rows = query_rows.reshape(KVH, groups * tok_rows, HD)
    attended = attention(query_rows, cache, fresh, length, shard_pos * tok_rows)
    attended = attended.reshape(KVH, groups, tok_rows, HD).transpose(2, 0, 1, 3)
    attended = attended.reshape(tok_rows, HEADS * HD)
    mid = (
        hidden_states.astype(jnp.float32)
        + jnp.dot(attended, w_out, preferred_element_type=jnp.float32)
    ).astype(jnp.bfloat16)
    normed2 = rms_scale(mid, ffn_gain)
    group_count = lax.axis_size("req")
    local_experts = w_gate.shape[0]
    expert_count = local_experts * group_count
    capacity = min(tok_rows, 5 * tok_rows * TOP // (4 * expert_count))
    logits = jnp.dot(normed2, w_router, preferred_element_type=jnp.float32)
    picked = expert_ids[:, :, None] == jnp.arange(expert_count, dtype=jnp.int32)[None, None, :]
    chosen = jnp.sum(jnp.where(picked, logits[:, None, :], 0.0), axis=-1)
    gates = jax.nn.softmax(chosen, axis=-1)
    flat_hot = picked.reshape(tok_rows * TOP, expert_count).astype(jnp.int32)
    ranks = jnp.cumsum(flat_hot, axis=0) - flat_hot
    slot_rank = jnp.sum(ranks * flat_hot, axis=-1)
    slots = expert_ids.reshape(-1) * capacity + slot_rank
    slot_table = (
        slots.reshape(tok_rows, TOP)[:, :, None]
        == jnp.arange(expert_count * capacity, dtype=jnp.int32)[None, None, :]
    )
    placing = jnp.any(slot_table, axis=1).astype(jnp.bfloat16)
    outgoing = jnp.einsum("ts,td->sd", placing, normed2, preferred_element_type=jnp.float32).astype(
        jnp.bfloat16
    )
    outgoing = outgoing.reshape(group_count, local_experts, capacity, D)
    arrived = lax.all_to_all(outgoing, "req", split_axis=0, concat_axis=0, tiled=True)
    weights = jnp.concatenate([w_gate, w_up, w_down], axis=-1)
    weights = lax.all_gather(weights, "shard", axis=1, tiled=True)
    gate_piece = weights[..., :D]
    up_piece = weights[..., D : 2 * D]
    down_piece = weights[..., 2 * D :]
    gate = jnp.einsum("sjcd,jhd->sjch", arrived, gate_piece, preferred_element_type=jnp.float32)
    upper = jnp.einsum("sjcd,jhd->sjch", arrived, up_piece, preferred_element_type=jnp.float32)
    inner = (jax.nn.silu(gate) * upper).astype(jnp.bfloat16)
    summed = jnp.einsum("sjch,jhd->sjcd", inner, down_piece, preferred_element_type=jnp.float32)
    returned = lax.all_to_all(
        summed.astype(jnp.bfloat16), "req", split_axis=0, concat_axis=0, tiled=True
    )
    returned = returned.reshape(expert_count * capacity, D)
    expert_rows = returned[slots].reshape(tok_rows, TOP, D)
    mixture = jnp.sum(gates[:, :, None] * expert_rows.astype(jnp.float32), axis=1)
    return (mid.astype(jnp.float32) + mixture).astype(jnp.bfloat16)


def solution(mesh):
    return jax.shard_map(
        local,
        mesh=mesh,
        in_specs=(
            P(("req", "shard"), None),
            P(),
            P(),
            P(),
            P("req", "shard", None),
            P("req"),
            P(),
            P(),
            P(("req", "shard"), None),
            P("req", "shard", None),
            P("req", "shard", None),
            P("req", "shard", None),
        ),
        out_specs=P(("req", "shard"), None),
        check_vma=False,
    )
```

```python
import functools
import math

import jax
import jax.numpy as jnp
from jax import lax
from jax.experimental import pallas as pl
from jax.experimental.pallas import tpu as pltpu
from jax.sharding import PartitionSpec as P

D = 1536
HEADS = 24
KVH = 8
HD = 64
TOP = 8


EPSILON = 1e-05
NEG_FILL = -1e30
FAR_LIMIT = 1 << 30
BLK = 512
NEG = NEG_FILL

def attn_kernel(meta_ref, q_ref, cache_ref, new_ref, o_ref, m_sc, l_sc, acc_sc, *, n_cache, rows):
    i = pl.program_id(0)
    length = meta_ref[0]
    qbase = meta_ref[1]

    @pl.when(i == 0)
    def _():
        m_sc[...] = jnp.full(m_sc.shape, NEG, jnp.float32)
        l_sc[...] = jnp.zeros(l_sc.shape, jnp.float32)
        acc_sc[...] = jnp.zeros(acc_sc.shape, jnp.float32)

    def step(kv_ref, allowed):
        for g in range(KVH):
            q = q_ref[g]
            k = kv_ref[:, g * HD:(g + 1) * HD]
            v = kv_ref[:, KVH * HD + g * HD:KVH * HD + (g + 1) * HD]
            s = lax.dot_general(q, k, (((1,), (1,)), ((), ())), preferred_element_type=jnp.float32) * (HD ** -0.5)
            s = jnp.where(allowed, s, NEG)
            m_prev = m_sc[g]
            m_new = jnp.maximum(m_prev, jnp.max(s, axis=-1, keepdims=True))
            p = jnp.where(allowed, jnp.exp(s - m_new), 0.0)
            factor = jnp.exp(m_prev - m_new)
            l_sc[g] = l_sc[g] * factor + jnp.sum(p, axis=-1, keepdims=True)
            acc_sc[g] = acc_sc[g] * factor + jnp.dot(p.astype(jnp.bfloat16), v, preferred_element_type=jnp.float32)
            m_sc[g] = m_new

    @pl.when((i < n_cache) & (i * BLK < length))
    def _():
        key = i * BLK + lax.broadcasted_iota(jnp.int32, (rows, BLK), 1)
        step(cache_ref, key < length)

    j = i - n_cache
    tok = rows // (HEADS // KVH)

    @pl.when((i >= n_cache) & (j * BLK <= qbase))
    def _():
        key = j * BLK + lax.broadcasted_iota(jnp.int32, (rows, BLK), 1)
        offset = key // tok
        qpos = lax.broadcasted_iota(jnp.int32, (rows, BLK), 0) % tok
        allowed = (offset * tok <= qbase) & ((offset > 0) | (key % tok <= qpos))
        step(new_ref, allowed)

    @pl.when(i == pl.num_programs(0) - 1)
    def _():
        for g in range(KVH):
            o_ref[g] = (acc_sc[g] / l_sc[g]).astype(o_ref.dtype)

def attention(queries, cache, new_kv, length, qbase):
    rows = queries.shape[1]
    n_cache = cache.shape[0] // BLK
    n_new = new_kv.shape[0] // BLK
    meta = jnp.stack([length, qbase]).astype(jnp.int32)
    kern = functools.partial(attn_kernel, n_cache=n_cache, rows=rows)
    return pl.pallas_call(
        kern,
        out_shape=jax.ShapeDtypeStruct((KVH, rows, HD), jnp.bfloat16),
        grid_spec=pltpu.PrefetchScalarGridSpec(
            num_scalar_prefetch=1,
            grid=(n_cache + n_new,),
            in_specs=[
                pl.BlockSpec((KVH, rows, HD), lambda i, m: (0, 0, 0)),
                pl.BlockSpec((BLK, 2 * KVH * HD), lambda i, m: (jnp.minimum(i, n_cache - 1), 0)),
                pl.BlockSpec((BLK, 2 * KVH * HD), lambda i, m: (jnp.maximum(i - n_cache, 0), 0)),
            ],
            out_specs=pl.BlockSpec((KVH, rows, HD), lambda i, m: (0, 0, 0)),
            scratch_shapes=[
                pltpu.VMEM((KVH, rows, 1), jnp.float32),
                pltpu.VMEM((KVH, rows, 1), jnp.float32),
                pltpu.VMEM((KVH, rows, HD), jnp.float32),
            ],
        ),
        compiler_params=pltpu.CompilerParams(dimension_semantics=("arbitrary",)),
    )(meta, queries, cache, new_kv)


def rms_scale(values, gain):
    floats = values.astype(jnp.float32)
    inverse = lax.rsqrt(jnp.mean(floats * floats, axis=-1, keepdims=True) + EPSILON)
    return (floats * inverse * gain).astype(jnp.bfloat16)


def rotate(values, positions):
    half_dim = values.shape[-1] // 2
    freqs = jnp.power(10000.0, -jnp.arange(half_dim, dtype=jnp.float32) / half_dim)
    angles = positions.astype(jnp.float32)[:, None] * freqs[None, :]
    cosine = jnp.cos(angles)[:, None, :]
    sine = jnp.sin(angles)[:, None, :]
    first = values[..., :half_dim]
    second = values[..., half_dim:]
    return jnp.concatenate(
        [first * cosine - second * sine, second * cosine + first * sine], axis=-1
    )


def local(
    hidden_states,
    attn_gain,
    w_qkv,
    w_out,
    kv_cache,
    cached_len,
    ffn_gain,
    w_router,
    expert_ids,
    w_gate,
    w_up,
    w_down,
):
    groups = HEADS // KVH
    tok_rows = hidden_states.shape[0]
    shard_pos = lax.axis_index("shard")
    length = cached_len[0]
    normed = rms_scale(hidden_states, attn_gain)
    qkv = jnp.dot(normed, w_qkv, preferred_element_type=jnp.float32)
    positions = length + shard_pos * tok_rows + jnp.arange(tok_rows, dtype=jnp.int32)
    queries = rotate(qkv[:, : HEADS * HD].reshape(tok_rows, HEADS, HD), positions).astype(
        jnp.bfloat16
    )
    new_keys = rotate(
        qkv[:, HEADS * HD : (HEADS + KVH) * HD].reshape(tok_rows, KVH, HD), positions
    ).astype(jnp.bfloat16)
    new_values = qkv[:, (HEADS + KVH) * HD :].astype(jnp.bfloat16)
    new_kv = jnp.concatenate([new_keys.reshape(tok_rows, KVH * HD), new_values], axis=1)
    cache = lax.all_gather(kv_cache[0], "shard", axis=0, tiled=True)
    shards = lax.axis_size("shard")
    fresh = [new_kv]
    for k in range(1, shards):
        pairs = [(s, s + k) for s in range(shards - k)]
        fresh.append(lax.ppermute(new_kv, "shard", pairs))
    fresh = jnp.concatenate(fresh, axis=0)
    query_rows = queries.reshape(tok_rows, KVH, groups, HD).transpose(1, 2, 0, 3)
    query_rows = query_rows.reshape(KVH, groups * tok_rows, HD)
    attended = attention(query_rows, cache, fresh, length, shard_pos * tok_rows)
    attended = attended.reshape(KVH, groups, tok_rows, HD).transpose(2, 0, 1, 3)
    attended = attended.reshape(tok_rows, HEADS * HD)
    mid = (
        hidden_states.astype(jnp.float32)
        + jnp.dot(attended, w_out, preferred_element_type=jnp.float32)
    ).astype(jnp.bfloat16)
    normed2 = rms_scale(mid, ffn_gain)
    group_count = lax.axis_size("req")
    local_experts = w_gate.shape[0]
    expert_count = local_experts * group_count
    capacity = min(tok_rows, 5 * tok_rows * TOP // (4 * expert_count))
    logits = jnp.dot(normed2, w_router, preferred_element_type=jnp.float32)
    picked = expert_ids[:, :, None] == jnp.arange(expert_count, dtype=jnp.int32)[None, None, :]
    chosen = jnp.sum(jnp.where(picked, logits[:, None, :], 0.0), axis=-1)
    gates = jax.nn.softmax(chosen, axis=-1)
    flat_hot = picked.reshape(tok_rows * TOP, expert_count).astype(jnp.int32)
    ranks = jnp.cumsum(flat_hot, axis=0) - flat_hot
    slot_rank = jnp.sum(ranks * flat_hot, axis=-1)
    slots = expert_ids.reshape(-1) * capacity + slot_rank
    slot_table = (
        slots.reshape(tok_rows, TOP)[:, :, None]
        == jnp.arange(expert_count * capacity, dtype=jnp.int32)[None, None, :]
    )
    placing = jnp.any(slot_table, axis=1).astype(jnp.bfloat16)
    outgoing = jnp.einsum("ts,td->sd", placing, normed2, preferred_element_type=jnp.float32).astype(
        jnp.bfloat16
    )
    outgoing = outgoing.reshape(group_count, local_experts, capacity, D)
    arrived = lax.all_to_all(outgoing, "req", split_axis=0, concat_axis=0, tiled=True)
    weights = jnp.concatenate([w_gate, w_up, w_down], axis=-1)
    weights = lax.all_gather(weights, "shard", axis=1, tiled=True)
    gate_piece = weights[..., :D]
    up_piece = weights[..., D : 2 * D]
    down_piece = weights[..., 2 * D :]
    gate = jnp.einsum("sjcd,jhd->sjch", arrived, gate_piece, preferred_element_type=jnp.float32)
    upper = jnp.einsum("sjcd,jhd->sjch", arrived, up_piece, preferred_element_type=jnp.float32)
    inner = (jax.nn.silu(gate) * upper).astype(jnp.bfloat16)
    summed = jnp.einsum("sjch,jhd->sjcd", inner, down_piece, preferred_element_type=jnp.float32)
    returned = lax.all_to_all(
        summed.astype(jnp.bfloat16), "req", split_axis=0, concat_axis=0, tiled=True
    )
    returned = returned.reshape(expert_count * capacity, D)
    expert_rows = returned[slots].reshape(tok_rows, TOP, D)
    mixture = jnp.sum(gates[:, :, None] * expert_rows.astype(jnp.float32), axis=1)
    return (mid.astype(jnp.float32) + mixture).astype(jnp.bfloat16)


def solution(mesh):
    return jax.shard_map(
        local,
        mesh=mesh,
        in_specs=(
            P(("req", "shard"), None),
            P(),
            P(),
            P(),
            P("req", "shard", None),
            P("req"),
            P(),
            P(),
            P(("req", "shard"), None),
            P("req", "shard", None),
            P("req", "shard", None),
            P("req", "shard", None),
        ),
        out_specs=P(("req", "shard"), None),
        check_vma=False,
    )
```

```python
import functools
import math

import jax
import jax.numpy as jnp
from jax import lax
from jax.experimental import pallas as pl
from jax.experimental.pallas import tpu as pltpu
from jax.sharding import PartitionSpec as P

D = 1536
HEADS = 24
KVH = 8
HD = 64
TOP = 8


EPSILON = 1e-05
NEG_FILL = -1e30
FAR_LIMIT = 1 << 30
BLK = 512
NEG = NEG_FILL

def attn_kernel(meta_ref, q_ref, cache_ref, new_ref, o_ref, m_sc, l_sc, acc_sc, *, n_cache, rows):
    i = pl.program_id(0)
    length = meta_ref[0]
    qbase = meta_ref[1]

    @pl.when(i == 0)
    def _():
        m_sc[...] = jnp.full(m_sc.shape, NEG, jnp.float32)
        l_sc[...] = jnp.zeros(l_sc.shape, jnp.float32)
        acc_sc[...] = jnp.zeros(acc_sc.shape, jnp.float32)

    def step(kv_ref, allowed):
        for g in range(KVH):
            q = q_ref[g]
            k = kv_ref[:, g * HD:(g + 1) * HD]
            v = kv_ref[:, KVH * HD + g * HD:KVH * HD + (g + 1) * HD]
            s = lax.dot_general(q, k, (((1,), (1,)), ((), ())), preferred_element_type=jnp.float32) * (HD ** -0.5)
            s = jnp.where(allowed, s, NEG)
            m_prev = m_sc[g]
            m_new = jnp.maximum(m_prev, jnp.max(s, axis=-1, keepdims=True))
            p = jnp.where(allowed, jnp.exp(s - m_new), 0.0)
            factor = jnp.exp(m_prev - m_new)
            l_sc[g] = l_sc[g] * factor + jnp.sum(p, axis=-1, keepdims=True)
            acc_sc[g] = acc_sc[g] * factor + jnp.dot(p.astype(jnp.bfloat16), v, preferred_element_type=jnp.float32)
            m_sc[g] = m_new

    @pl.when((i < n_cache) & (i * BLK < length))
    def _():
        key = i * BLK + lax.broadcasted_iota(jnp.int32, (rows, BLK), 1)
        step(cache_ref, key < length)

    j = i - n_cache
    tok = rows // (HEADS // KVH)

    @pl.when((i >= n_cache) & (j * BLK <= qbase))
    def _():
        key = j * BLK + lax.broadcasted_iota(jnp.int32, (rows, BLK), 1)
        offset = key // tok
        qpos = lax.broadcasted_iota(jnp.int32, (rows, BLK), 0) % tok
        allowed = (offset * tok <= qbase) & ((offset > 0) | (key % tok <= qpos))
        step(new_ref, allowed)

    @pl.when(i == pl.num_programs(0) - 1)
    def _():
        for g in range(KVH):
            o_ref[g] = (acc_sc[g] / l_sc[g]).astype(o_ref.dtype)

def attention(queries, cache, new_kv, length, qbase):
    rows = queries.shape[1]
    n_cache = cache.shape[0] // BLK
    n_new = new_kv.shape[0] // BLK
    meta = jnp.stack([length, qbase]).astype(jnp.int32)
    kern = functools.partial(attn_kernel, n_cache=n_cache, rows=rows)
    return pl.pallas_call(
        kern,
        out_shape=jax.ShapeDtypeStruct((KVH, rows, HD), jnp.bfloat16),
        grid_spec=pltpu.PrefetchScalarGridSpec(
            num_scalar_prefetch=1,
            grid=(n_cache + n_new,),
            in_specs=[
                pl.BlockSpec((KVH, rows, HD), lambda i, m: (0, 0, 0)),
                pl.BlockSpec((BLK, 2 * KVH * HD), lambda i, m: (jnp.minimum(i, n_cache - 1), 0)),
                pl.BlockSpec((BLK, 2 * KVH * HD), lambda i, m: (jnp.maximum(i - n_cache, 0), 0)),
            ],
            out_specs=pl.BlockSpec((KVH, rows, HD), lambda i, m: (0, 0, 0)),
            scratch_shapes=[
                pltpu.VMEM((KVH, rows, 1), jnp.float32),
                pltpu.VMEM((KVH, rows, 1), jnp.float32),
                pltpu.VMEM((KVH, rows, HD), jnp.float32),
            ],
        ),
        compiler_params=pltpu.CompilerParams(dimension_semantics=("arbitrary",)),
    )(meta, queries, cache, new_kv)


def rms_scale(values, gain):
    floats = values.astype(jnp.float32)
    inverse = lax.rsqrt(jnp.mean(floats * floats, axis=-1, keepdims=True) + EPSILON)
    return (floats * inverse * gain).astype(jnp.bfloat16)


def rotate(values, positions):
    half_dim = values.shape[-1] // 2
    freqs = jnp.power(10000.0, -jnp.arange(half_dim, dtype=jnp.float32) / half_dim)
    angles = positions.astype(jnp.float32)[:, None] * freqs[None, :]
    cosine = jnp.cos(angles)[:, None, :]
    sine = jnp.sin(angles)[:, None, :]
    first = values[..., :half_dim]
    second = values[..., half_dim:]
    return jnp.concatenate(
        [first * cosine - second * sine, second * cosine + first * sine], axis=-1
    )


def local(
    hidden_states,
    attn_gain,
    w_qkv,
    w_out,
    kv_cache,
    cached_len,
    ffn_gain,
    w_router,
    expert_ids,
    w_gate,
    w_up,
    w_down,
):
    groups = HEADS // KVH
    tok_rows = hidden_states.shape[0]
    shard_pos = lax.axis_index("shard")
    length = cached_len[0]
    normed = rms_scale(hidden_states, attn_gain)
    qkv = jnp.dot(normed, w_qkv, preferred_element_type=jnp.float32)
    positions = length + shard_pos * tok_rows + jnp.arange(tok_rows, dtype=jnp.int32)
    queries = rotate(qkv[:, : HEADS * HD].reshape(tok_rows, HEADS, HD), positions).astype(
        jnp.bfloat16
    )
    new_keys = rotate(
        qkv[:, HEADS * HD : (HEADS + KVH) * HD].reshape(tok_rows, KVH, HD), positions
    ).astype(jnp.bfloat16)
    new_values = qkv[:, (HEADS + KVH) * HD :].astype(jnp.bfloat16)
    new_kv = jnp.concatenate([new_keys.reshape(tok_rows, KVH * HD), new_values], axis=1)
    cache = lax.all_gather(kv_cache[0], "shard", axis=0, tiled=True)
    shards = lax.axis_size("shard")
    fresh = [new_kv]
    for k in range(1, shards):
        pairs = [(s, s + k) for s in range(shards - k)]
        fresh.append(lax.ppermute(new_kv, "shard", pairs))
    fresh = jnp.concatenate(fresh, axis=0)
    query_rows = queries.reshape(tok_rows, KVH, groups, HD).transpose(1, 2, 0, 3)
    query_rows = query_rows.reshape(KVH, groups * tok_rows, HD)
    attended = attention(query_rows, cache, fresh, length, shard_pos * tok_rows)
    attended = attended.reshape(KVH, groups, tok_rows, HD).transpose(2, 0, 1, 3)
    attended = attended.reshape(tok_rows, HEADS * HD)
    mid = (
        hidden_states.astype(jnp.float32)
        + jnp.dot(attended, w_out, preferred_element_type=jnp.float32)
    ).astype(jnp.bfloat16)
    normed2 = rms_scale(mid, ffn_gain)
    group_count = lax.axis_size("req")
    local_experts = w_gate.shape[0]
    expert_count = local_experts * group_count
    capacity = min(tok_rows, 5 * tok_rows * TOP // (4 * expert_count))
    logits = jnp.dot(normed2, w_router, preferred_element_type=jnp.float32)
    picked = expert_ids[:, :, None] == jnp.arange(expert_count, dtype=jnp.int32)[None, None, :]
    chosen = jnp.sum(jnp.where(picked, logits[:, None, :], 0.0), axis=-1)
    gates = jax.nn.softmax(chosen, axis=-1)
    flat_hot = picked.reshape(tok_rows * TOP, expert_count).astype(jnp.int32)
    ranks = jnp.cumsum(flat_hot, axis=0) - flat_hot
    slot_rank = jnp.sum(ranks * flat_hot, axis=-1)
    slots = expert_ids.reshape(-1) * capacity + slot_rank
    slot_table = (
        slots.reshape(tok_rows, TOP)[:, :, None]
        == jnp.arange(expert_count * capacity, dtype=jnp.int32)[None, None, :]
    )
    placing = jnp.any(slot_table, axis=1).astype(jnp.bfloat16)
    outgoing = jnp.einsum("ts,td->sd", placing, normed2, preferred_element_type=jnp.float32).astype(
        jnp.bfloat16
    )
    outgoing = outgoing.reshape(group_count, local_experts, capacity, D)
    arrived = lax.all_to_all(outgoing, "req", split_axis=0, concat_axis=0, tiled=True)
    weights = jnp.concatenate([w_gate, w_up, w_down], axis=-1)
    returned = []
    for j in range(local_experts):
        piece = lax.all_gather(weights[j], "shard", axis=0, tiled=True)
        rows_in = arrived[:, j]
        gate = jnp.einsum("scd,hd->sch", rows_in, piece[:, :D], preferred_element_type=jnp.float32)
        upper = jnp.einsum("scd,hd->sch", rows_in, piece[:, D : 2 * D], preferred_element_type=jnp.float32)
        inner = (jax.nn.silu(gate) * upper).astype(jnp.bfloat16)
        summed = jnp.einsum("sch,hd->scd", inner, piece[:, 2 * D :], preferred_element_type=jnp.float32)
        returned.append(
            lax.all_to_all(summed.astype(jnp.bfloat16), "req", split_axis=0, concat_axis=0, tiled=True)
        )
    returned = jnp.stack(returned, axis=1)
    returned = returned.reshape(expert_count * capacity, D)
    expert_rows = returned[slots].reshape(tok_rows, TOP, D)
    mixture = jnp.sum(gates[:, :, None] * expert_rows.astype(jnp.float32), axis=1)
    return (mid.astype(jnp.float32) + mixture).astype(jnp.bfloat16)


def solution(mesh):
    return jax.shard_map(
        local,
        mesh=mesh,
        in_specs=(
            P(("req", "shard"), None),
            P(),
            P(),
            P(),
            P("req", "shard", None),
            P("req"),
            P(),
            P(),
            P(("req", "shard"), None),
            P("req", "shard", None),
            P("req", "shard", None),
            P("req", "shard", None),
        ),
        out_specs=P(("req", "shard"), None),
        check_vma=False,
    )
```

```python
import functools
import math

import jax
import jax.numpy as jnp
from jax import lax
from jax.experimental import pallas as pl
from jax.experimental.pallas import tpu as pltpu
from jax.sharding import PartitionSpec as P

D = 1536
HEADS = 24
KVH = 8
HD = 64
TOP = 8


EPSILON = 1e-05
NEG_FILL = -1e30
FAR_LIMIT = 1 << 30
BLK = 512
NEG = NEG_FILL

def attn_kernel(meta_ref, q_ref, cache_ref, new_ref, o_ref, m_sc, l_sc, acc_sc, *, n_cache, rows):
    i = pl.program_id(0)
    length = meta_ref[0]
    qbase = meta_ref[1]

    @pl.when(i == 0)
    def _():
        m_sc[...] = jnp.full(m_sc.shape, NEG, jnp.float32)
        l_sc[...] = jnp.zeros(l_sc.shape, jnp.float32)
        acc_sc[...] = jnp.zeros(acc_sc.shape, jnp.float32)

    def step(kv_ref, allowed):
        for g in range(KVH):
            q = q_ref[g]
            k = kv_ref[:, g * HD:(g + 1) * HD]
            v = kv_ref[:, KVH * HD + g * HD:KVH * HD + (g + 1) * HD]
            s = lax.dot_general(q, k, (((1,), (1,)), ((), ())), preferred_element_type=jnp.float32) * (HD ** -0.5)
            s = jnp.where(allowed, s, NEG)
            m_prev = m_sc[g]
            m_new = jnp.maximum(m_prev, jnp.max(s, axis=-1, keepdims=True))
            p = jnp.where(allowed, jnp.exp(s - m_new), 0.0)
            factor = jnp.exp(m_prev - m_new)
            l_sc[g] = l_sc[g] * factor + jnp.sum(p, axis=-1, keepdims=True)
            acc_sc[g] = acc_sc[g] * factor + jnp.dot(p.astype(jnp.bfloat16), v, preferred_element_type=jnp.float32)
            m_sc[g] = m_new

    own = meta_ref[2]
    shards = meta_ref[3]
    chunk = n_cache * BLK // shards
    first = (own - (i * BLK) // chunk + shards) % shards
    second = (own - (i * BLK + BLK - 1) // chunk + shards) % shards

    @pl.when((i < n_cache) & ((first * chunk < length) | (second * chunk < length)))
    def _():
        key = i * BLK + lax.broadcasted_iota(jnp.int32, (rows, BLK), 1)
        source = (own - key // chunk + shards) % shards
        step(cache_ref, source * chunk + key % chunk < length)

    j = i - n_cache
    tok = rows // (HEADS // KVH)

    @pl.when((i >= n_cache) & (j * BLK <= qbase))
    def _():
        key = j * BLK + lax.broadcasted_iota(jnp.int32, (rows, BLK), 1)
        offset = key // tok
        qpos = lax.broadcasted_iota(jnp.int32, (rows, BLK), 0) % tok
        allowed = (offset * tok <= qbase) & ((offset > 0) | (key % tok <= qpos))
        step(new_ref, allowed)

    @pl.when(i == pl.num_programs(0) - 1)
    def _():
        for g in range(KVH):
            o_ref[g] = (acc_sc[g] / l_sc[g]).astype(o_ref.dtype)

def attention(queries, cache, new_kv, length, qbase, own, shards):
    rows = queries.shape[1]
    n_cache = cache.shape[0] // BLK
    n_new = new_kv.shape[0] // BLK
    meta = jnp.stack([length, qbase, own, jnp.int32(shards)]).astype(jnp.int32)
    kern = functools.partial(attn_kernel, n_cache=n_cache, rows=rows)
    return pl.pallas_call(
        kern,
        out_shape=jax.ShapeDtypeStruct((KVH, rows, HD), jnp.bfloat16),
        grid_spec=pltpu.PrefetchScalarGridSpec(
            num_scalar_prefetch=1,
            grid=(n_cache + n_new,),
            in_specs=[
                pl.BlockSpec((KVH, rows, HD), lambda i, m: (0, 0, 0)),
                pl.BlockSpec((BLK, 2 * KVH * HD), lambda i, m: (jnp.minimum(i, n_cache - 1), 0)),
                pl.BlockSpec((BLK, 2 * KVH * HD), lambda i, m: (jnp.maximum(i - n_cache, 0), 0)),
            ],
            out_specs=pl.BlockSpec((KVH, rows, HD), lambda i, m: (0, 0, 0)),
            scratch_shapes=[
                pltpu.VMEM((KVH, rows, 1), jnp.float32),
                pltpu.VMEM((KVH, rows, 1), jnp.float32),
                pltpu.VMEM((KVH, rows, HD), jnp.float32),
            ],
        ),
        compiler_params=pltpu.CompilerParams(dimension_semantics=("arbitrary",)),
    )(meta, queries, cache, new_kv)


def rms_scale(values, gain):
    floats = values.astype(jnp.float32)
    inverse = lax.rsqrt(jnp.mean(floats * floats, axis=-1, keepdims=True) + EPSILON)
    return (floats * inverse * gain).astype(jnp.bfloat16)


def rotate(values, positions):
    half_dim = values.shape[-1] // 2
    freqs = jnp.power(10000.0, -jnp.arange(half_dim, dtype=jnp.float32) / half_dim)
    angles = positions.astype(jnp.float32)[:, None] * freqs[None, :]
    cosine = jnp.cos(angles)[:, None, :]
    sine = jnp.sin(angles)[:, None, :]
    first = values[..., :half_dim]
    second = values[..., half_dim:]
    return jnp.concatenate(
        [first * cosine - second * sine, second * cosine + first * sine], axis=-1
    )


def local(
    hidden_states,
    attn_gain,
    w_qkv,
    w_out,
    kv_cache,
    cached_len,
    ffn_gain,
    w_router,
    expert_ids,
    w_gate,
    w_up,
    w_down,
):
    groups = HEADS // KVH
    tok_rows = hidden_states.shape[0]
    shard_pos = lax.axis_index("shard")
    length = cached_len[0]
    normed = rms_scale(hidden_states, attn_gain)
    qkv = jnp.dot(normed, w_qkv, preferred_element_type=jnp.float32)
    positions = length + shard_pos * tok_rows + jnp.arange(tok_rows, dtype=jnp.int32)
    queries = rotate(qkv[:, : HEADS * HD].reshape(tok_rows, HEADS, HD), positions).astype(
        jnp.bfloat16
    )
    new_keys = rotate(
        qkv[:, HEADS * HD : (HEADS + KVH) * HD].reshape(tok_rows, KVH, HD), positions
    ).astype(jnp.bfloat16)
    new_values = qkv[:, (HEADS + KVH) * HD :].astype(jnp.bfloat16)
    new_kv = jnp.concatenate([new_keys.reshape(tok_rows, KVH * HD), new_values], axis=1)
    shards = lax.axis_size("shard")
    cache = [kv_cache[0]]
    for k in range(1, shards):
        pairs = [(s, (s + k) % shards) for s in range(shards)]
        cache.append(lax.ppermute(kv_cache[0], "shard", pairs))
    cache = jnp.concatenate(cache, axis=0)
    fresh = [new_kv]
    for k in range(1, shards):
        pairs = [(s, s + k) for s in range(shards - k)]
        fresh.append(lax.ppermute(new_kv, "shard", pairs))
    fresh = jnp.concatenate(fresh, axis=0)
    query_rows = queries.reshape(tok_rows, KVH, groups, HD).transpose(1, 2, 0, 3)
    query_rows = query_rows.reshape(KVH, groups * tok_rows, HD)
    attended = attention(query_rows, cache, fresh, length, shard_pos * tok_rows, shard_pos, shards)
    attended = attended.reshape(KVH, groups, tok_rows, HD).transpose(2, 0, 1, 3)
    attended = attended.reshape(tok_rows, HEADS * HD)
    mid = (
        hidden_states.astype(jnp.float32)
        + jnp.dot(attended, w_out, preferred_element_type=jnp.float32)
    ).astype(jnp.bfloat16)
    normed2 = rms_scale(mid, ffn_gain)
    group_count = lax.axis_size("req")
    local_experts = w_gate.shape[0]
    expert_count = local_experts * group_count
    capacity = min(tok_rows, 5 * tok_rows * TOP // (4 * expert_count))
    logits = jnp.dot(normed2, w_router, preferred_element_type=jnp.float32)
    picked = expert_ids[:, :, None] == jnp.arange(expert_count, dtype=jnp.int32)[None, None, :]
    chosen = jnp.sum(jnp.where(picked, logits[:, None, :], 0.0), axis=-1)
    gates = jax.nn.softmax(chosen, axis=-1)
    flat_hot = picked.reshape(tok_rows * TOP, expert_count).astype(jnp.int32)
    ranks = jnp.cumsum(flat_hot, axis=0) - flat_hot
    slot_rank = jnp.sum(ranks * flat_hot, axis=-1)
    slots = expert_ids.reshape(-1) * capacity + slot_rank
    slot_table = (
        slots.reshape(tok_rows, TOP)[:, :, None]
        == jnp.arange(expert_count * capacity, dtype=jnp.int32)[None, None, :]
    )
    placing = jnp.any(slot_table, axis=1).astype(jnp.bfloat16)
    outgoing = jnp.einsum("ts,td->sd", placing, normed2, preferred_element_type=jnp.float32).astype(
        jnp.bfloat16
    )
    outgoing = outgoing.reshape(group_count, local_experts, capacity, D)
    arrived = lax.all_to_all(outgoing, "req", split_axis=0, concat_axis=0, tiled=True)
    weights = jnp.concatenate([w_gate, w_up, w_down], axis=-1)
    weights = lax.all_gather(weights, "shard", axis=1, tiled=True)
    gate_piece = weights[..., :D]
    up_piece = weights[..., D : 2 * D]
    down_piece = weights[..., 2 * D :]
    gate = jnp.einsum("sjcd,jhd->sjch", arrived, gate_piece, preferred_element_type=jnp.float32)
    upper = jnp.einsum("sjcd,jhd->sjch", arrived, up_piece, preferred_element_type=jnp.float32)
    inner = (jax.nn.silu(gate) * upper).astype(jnp.bfloat16)
    summed = jnp.einsum("sjch,jhd->sjcd", inner, down_piece, preferred_element_type=jnp.float32)
    returned = lax.all_to_all(
        summed.astype(jnp.bfloat16), "req", split_axis=0, concat_axis=0, tiled=True
    )
    returned = returned.reshape(expert_count * capacity, D)
    expert_rows = returned[slots].reshape(tok_rows, TOP, D)
    mixture = jnp.sum(gates[:, :, None] * expert_rows.astype(jnp.float32), axis=1)
    return (mid.astype(jnp.float32) + mixture).astype(jnp.bfloat16)


def solution(mesh):
    return jax.shard_map(
        local,
        mesh=mesh,
        in_specs=(
            P(("req", "shard"), None),
            P(),
            P(),
            P(),
            P("req", "shard", None),
            P("req"),
            P(),
            P(),
            P(("req", "shard"), None),
            P("req", "shard", None),
            P("req", "shard", None),
            P("req", "shard", None),
        ),
        out_specs=P(("req", "shard"), None),
        check_vma=False,
    )
```

```python
import functools
import math

import jax
import jax.numpy as jnp
from jax import lax
from jax.experimental import pallas as pl
from jax.experimental.pallas import tpu as pltpu
from jax.sharding import PartitionSpec as P

D = 1536
HEADS = 24
KVH = 8
HD = 64
TOP = 8


EPSILON = 1e-05
NEG_FILL = -1e30
FAR_LIMIT = 1 << 30
BLK = 512
NEG = NEG_FILL

def attn_kernel(meta_ref, q_ref, cache_ref, new_ref, o_ref, m_sc, l_sc, acc_sc, *, n_cache, rows):
    i = pl.program_id(0)
    length = meta_ref[0]
    qbase = meta_ref[1]

    @pl.when(i == 0)
    def _():
        m_sc[...] = jnp.full(m_sc.shape, NEG, jnp.float32)
        l_sc[...] = jnp.zeros(l_sc.shape, jnp.float32)
        acc_sc[...] = jnp.zeros(acc_sc.shape, jnp.float32)

    def step(kv_ref, allowed):
        for g in range(KVH):
            q = q_ref[g]
            k = kv_ref[:, g * HD:(g + 1) * HD]
            v = kv_ref[:, KVH * HD + g * HD:KVH * HD + (g + 1) * HD]
            s = lax.dot_general(q, k, (((1,), (1,)), ((), ())), preferred_element_type=jnp.float32) * (HD ** -0.5)
            s = jnp.where(allowed, s, NEG)
            m_prev = m_sc[g]
            m_new = jnp.maximum(m_prev, jnp.max(s, axis=-1, keepdims=True))
            p = jnp.where(allowed, jnp.exp(s - m_new), 0.0)
            factor = jnp.exp(m_prev - m_new)
            l_sc[g] = l_sc[g] * factor + jnp.sum(p, axis=-1, keepdims=True)
            acc_sc[g] = acc_sc[g] * factor + jnp.dot(p.astype(jnp.bfloat16), v, preferred_element_type=jnp.float32)
            m_sc[g] = m_new

    @pl.when((i < n_cache) & (i * BLK < length))
    def _():
        key = i * BLK + lax.broadcasted_iota(jnp.int32, (rows, BLK), 1)
        step(cache_ref, key < length)

    j = i - n_cache
    tok = rows // (HEADS // KVH)

    @pl.when((i >= n_cache) & (j * BLK <= qbase))
    def _():
        key = j * BLK + lax.broadcasted_iota(jnp.int32, (rows, BLK), 1)
        offset = key // tok
        qpos = lax.broadcasted_iota(jnp.int32, (rows, BLK), 0) % tok
        allowed = (offset * tok <= qbase) & ((offset > 0) | (key % tok <= qpos))
        step(new_ref, allowed)

    @pl.when(i == pl.num_programs(0) - 1)
    def _():
        for g in range(KVH):
            o_ref[g] = (acc_sc[g] / l_sc[g]).astype(o_ref.dtype)

def attention(queries, cache, new_kv, length, qbase):
    rows = queries.shape[1]
    n_cache = cache.shape[0] // BLK
    n_new = new_kv.shape[0] // BLK
    meta = jnp.stack([length, qbase]).astype(jnp.int32)
    kern = functools.partial(attn_kernel, n_cache=n_cache, rows=rows)
    return pl.pallas_call(
        kern,
        out_shape=jax.ShapeDtypeStruct((KVH, rows, HD), jnp.bfloat16),
        grid_spec=pltpu.PrefetchScalarGridSpec(
            num_scalar_prefetch=1,
            grid=(n_cache + n_new,),
            in_specs=[
                pl.BlockSpec((KVH, rows, HD), lambda i, m: (0, 0, 0)),
                pl.BlockSpec((BLK, 2 * KVH * HD), lambda i, m: (jnp.minimum(i, n_cache - 1), 0)),
                pl.BlockSpec((BLK, 2 * KVH * HD), lambda i, m: (jnp.maximum(i - n_cache, 0), 0)),
            ],
            out_specs=pl.BlockSpec((KVH, rows, HD), lambda i, m: (0, 0, 0)),
            scratch_shapes=[
                pltpu.VMEM((KVH, rows, 1), jnp.float32),
                pltpu.VMEM((KVH, rows, 1), jnp.float32),
                pltpu.VMEM((KVH, rows, HD), jnp.float32),
            ],
        ),
        compiler_params=pltpu.CompilerParams(dimension_semantics=("arbitrary",)),
    )(meta, queries, cache, new_kv)


def rms_scale(values, gain):
    floats = values.astype(jnp.float32)
    inverse = lax.rsqrt(jnp.mean(floats * floats, axis=-1, keepdims=True) + EPSILON)
    return (floats * inverse * gain).astype(jnp.bfloat16)


def rotate(values, positions):
    half_dim = values.shape[-1] // 2
    freqs = jnp.power(10000.0, -jnp.arange(half_dim, dtype=jnp.float32) / half_dim)
    angles = positions.astype(jnp.float32)[:, None] * freqs[None, :]
    cosine = jnp.cos(angles)[:, None, :]
    sine = jnp.sin(angles)[:, None, :]
    first = values[..., :half_dim]
    second = values[..., half_dim:]
    return jnp.concatenate(
        [first * cosine - second * sine, second * cosine + first * sine], axis=-1
    )


def local(
    hidden_states,
    attn_gain,
    w_qkv,
    w_out,
    kv_cache,
    cached_len,
    ffn_gain,
    w_router,
    expert_ids,
    w_gate,
    w_up,
    w_down,
):
    groups = HEADS // KVH
    tok_rows = hidden_states.shape[0]
    shard_pos = lax.axis_index("shard")
    length = cached_len[0]
    normed = rms_scale(hidden_states, attn_gain)
    qkv = jnp.dot(normed, w_qkv, preferred_element_type=jnp.float32)
    positions = length + shard_pos * tok_rows + jnp.arange(tok_rows, dtype=jnp.int32)
    queries = rotate(qkv[:, : HEADS * HD].reshape(tok_rows, HEADS, HD), positions).astype(
        jnp.bfloat16
    )
    new_keys = rotate(
        qkv[:, HEADS * HD : (HEADS + KVH) * HD].reshape(tok_rows, KVH, HD), positions
    ).astype(jnp.bfloat16)
    new_values = qkv[:, (HEADS + KVH) * HD :].astype(jnp.bfloat16)
    new_kv = jnp.concatenate([new_keys.reshape(tok_rows, KVH * HD), new_values], axis=1)
    cache = lax.all_gather(kv_cache[0], "shard", axis=0, tiled=True)
    shards = lax.axis_size("shard")
    fresh = [new_kv]
    for k in range(1, shards):
        pairs = [(s, s + k) for s in range(shards - k)]
        fresh.append(lax.ppermute(new_kv, "shard", pairs))
    fresh = jnp.concatenate(fresh, axis=0)
    query_rows = queries.reshape(tok_rows, KVH, groups, HD).transpose(1, 2, 0, 3)
    query_rows = query_rows.reshape(KVH, groups * tok_rows, HD)
    attended = attention(query_rows, cache, fresh, length, shard_pos * tok_rows)
    attended = attended.reshape(KVH, groups, tok_rows, HD).transpose(2, 0, 1, 3)
    attended = attended.reshape(tok_rows, HEADS * HD)
    mid = (
        hidden_states.astype(jnp.float32)
        + jnp.dot(attended, w_out, preferred_element_type=jnp.float32)
    ).astype(jnp.bfloat16)
    normed2 = rms_scale(mid, ffn_gain)
    group_count = lax.axis_size("req")
    local_experts = w_gate.shape[0]
    expert_count = local_experts * group_count
    capacity = min(tok_rows, 5 * tok_rows * TOP // (4 * expert_count))
    logits = jnp.dot(normed2, w_router, preferred_element_type=jnp.float32)
    picked = expert_ids[:, :, None] == jnp.arange(expert_count, dtype=jnp.int32)[None, None, :]
    chosen = jnp.sum(jnp.where(picked, logits[:, None, :], 0.0), axis=-1)
    gates = jax.nn.softmax(chosen, axis=-1)
    flat_hot = picked.reshape(tok_rows * TOP, expert_count).astype(jnp.int32)
    ranks = jnp.cumsum(flat_hot, axis=0) - flat_hot
    slot_rank = jnp.sum(ranks * flat_hot, axis=-1)
    slots = expert_ids.reshape(-1) * capacity + slot_rank
    slot_table = (
        slots.reshape(tok_rows, TOP)[:, :, None]
        == jnp.arange(expert_count * capacity, dtype=jnp.int32)[None, None, :]
    )
    placing = jnp.any(slot_table, axis=1).astype(jnp.bfloat16)
    outgoing = jnp.einsum("ts,td->sd", placing, normed2, preferred_element_type=jnp.float32).astype(
        jnp.bfloat16
    )
    outgoing = outgoing.reshape(group_count, local_experts, capacity, D)
    arrived = lax.all_to_all(outgoing, "req", split_axis=0, concat_axis=0, tiled=True)
    token_of = jnp.repeat(jnp.arange(tok_rows, dtype=jnp.float32), TOP)
    tags = jnp.zeros((expert_count * capacity, 2), jnp.float32)
    tags = tags.at[:, 0].set(-1.0).at[slots].set(jnp.stack([token_of, gates.reshape(-1)], axis=-1))
    tags = tags.reshape(group_count, local_experts * capacity, 2)
    tags = lax.all_to_all(tags, "req", split_axis=0, concat_axis=0, tiled=True)
    weights = jnp.concatenate([w_gate, w_up, w_down], axis=-1)
    weights = lax.all_gather(weights, "shard", axis=1, tiled=True)
    gate_piece = weights[..., :D]
    up_piece = weights[..., D : 2 * D]
    down_piece = weights[..., 2 * D :]
    gate = jnp.einsum("sjcd,jhd->sjch", arrived, gate_piece, preferred_element_type=jnp.float32)
    upper = jnp.einsum("sjcd,jhd->sjch", arrived, up_piece, preferred_element_type=jnp.float32)
    inner = (jax.nn.silu(gate) * upper).astype(jnp.bfloat16)
    summed = jnp.einsum("sjch,jhd->sjcd", inner, down_piece, preferred_element_type=jnp.float32)
    expert_rows = summed.astype(jnp.bfloat16).astype(jnp.float32)
    expert_rows = expert_rows.reshape(group_count, local_experts * capacity, D)
    owner = tags[..., 0].astype(jnp.int32)
    weighting = jnp.where(
        owner[:, None, :] == jnp.arange(tok_rows, dtype=jnp.int32)[None, :, None], tags[:, None, :, 1], 0.0
    )
    partial = jnp.einsum(
        "stm,smd->std", weighting, expert_rows, preferred_element_type=jnp.float32,
        precision=lax.Precision.HIGHEST,
    )
    returned = lax.all_to_all(partial.astype(jnp.bfloat16), "req", split_axis=0, concat_axis=0, tiled=True)
    mixture = jnp.sum(returned.astype(jnp.float32), axis=0)
    return (mid.astype(jnp.float32) + mixture).astype(jnp.bfloat16)


def solution(mesh):
    return jax.shard_map(
        local,
        mesh=mesh,
        in_specs=(
            P(("req", "shard"), None),
            P(),
            P(),
            P(),
            P("req", "shard", None),
            P("req"),
            P(),
            P(),
            P(("req", "shard"), None),
            P("req", "shard", None),
            P("req", "shard", None),
            P("req", "shard", None),
        ),
        out_specs=P(("req", "shard"), None),
        check_vma=False,
    )
```

```python
import functools
import math

import jax
import jax.numpy as jnp
from jax import lax
from jax.experimental import pallas as pl
from jax.experimental.pallas import tpu as pltpu
from jax.sharding import PartitionSpec as P

D = 1536
HEADS = 24
KVH = 8
HD = 64
TOP = 8


EPSILON = 1e-05
NEG_FILL = -1e30
FAR_LIMIT = 1 << 30
BLK = 512
NEG = NEG_FILL

def attn_kernel(meta_ref, q_ref, cache_ref, new_ref, o_ref, m_sc, l_sc, acc_sc, *, n_cache, rows):
    i = pl.program_id(0)
    length = meta_ref[0]
    qbase = meta_ref[1]

    @pl.when(i == 0)
    def _():
        m_sc[...] = jnp.full(m_sc.shape, NEG, jnp.float32)
        l_sc[...] = jnp.zeros(l_sc.shape, jnp.float32)
        acc_sc[...] = jnp.zeros(acc_sc.shape, jnp.float32)

    def step(kv_ref, allowed):
        for g in range(KVH):
            q = q_ref[g]
            k = kv_ref[:, g * HD:(g + 1) * HD]
            v = kv_ref[:, KVH * HD + g * HD:KVH * HD + (g + 1) * HD]
            s = lax.dot_general(q, k, (((1,), (1,)), ((), ())), preferred_element_type=jnp.float32) * (HD ** -0.5)
            s = jnp.where(allowed, s, NEG)
            m_prev = m_sc[g]
            m_new = jnp.maximum(m_prev, jnp.max(s, axis=-1, keepdims=True))
            p = jnp.where(allowed, jnp.exp(s - m_new), 0.0)
            factor = jnp.exp(m_prev - m_new)
            l_sc[g] = l_sc[g] * factor + jnp.sum(p, axis=-1, keepdims=True)
            acc_sc[g] = acc_sc[g] * factor + jnp.dot(p.astype(jnp.bfloat16), v, preferred_element_type=jnp.float32)
            m_sc[g] = m_new

    @pl.when((i < n_cache) & (i * BLK < length))
    def _():
        key = i * BLK + lax.broadcasted_iota(jnp.int32, (rows, BLK), 1)
        step(cache_ref, key < length)

    j = i - n_cache
    tok = rows // (HEADS // KVH)

    @pl.when((i >= n_cache) & (j * BLK <= qbase))
    def _():
        key = j * BLK + lax.broadcasted_iota(jnp.int32, (rows, BLK), 1)
        offset = key // tok
        qpos = lax.broadcasted_iota(jnp.int32, (rows, BLK), 0) % tok
        allowed = (offset * tok <= qbase) & ((offset > 0) | (key % tok <= qpos))
        step(new_ref, allowed)

    @pl.when(i == pl.num_programs(0) - 1)
    def _():
        for g in range(KVH):
            o_ref[g] = (acc_sc[g] / l_sc[g]).astype(o_ref.dtype)

def attention(queries, cache, new_kv, length, qbase):
    rows = queries.shape[1]
    n_cache = cache.shape[0] // BLK
    n_new = new_kv.shape[0] // BLK
    meta = jnp.stack([length, qbase]).astype(jnp.int32)
    kern = functools.partial(attn_kernel, n_cache=n_cache, rows=rows)
    return pl.pallas_call(
        kern,
        out_shape=jax.ShapeDtypeStruct((KVH, rows, HD), jnp.bfloat16),
        grid_spec=pltpu.PrefetchScalarGridSpec(
            num_scalar_prefetch=1,
            grid=(n_cache + n_new,),
            in_specs=[
                pl.BlockSpec((KVH, rows, HD), lambda i, m: (0, 0, 0)),
                pl.BlockSpec((BLK, 2 * KVH * HD), lambda i, m: (jnp.minimum(i, n_cache - 1), 0)),
                pl.BlockSpec((BLK, 2 * KVH * HD), lambda i, m: (jnp.maximum(i - n_cache, 0), 0)),
            ],
            out_specs=pl.BlockSpec((KVH, rows, HD), lambda i, m: (0, 0, 0)),
            scratch_shapes=[
                pltpu.VMEM((KVH, rows, 1), jnp.float32),
                pltpu.VMEM((KVH, rows, 1), jnp.float32),
                pltpu.VMEM((KVH, rows, HD), jnp.float32),
            ],
        ),
        compiler_params=pltpu.CompilerParams(dimension_semantics=("arbitrary",)),
    )(meta, queries, cache, new_kv)


def ffn_kernel(x_ref, w_ref, o_ref):
    rows = x_ref.shape[0] * x_ref.shape[2]
    x = x_ref[...].reshape(rows, D)
    w = w_ref[0]
    dims = (((1,), (1,)), ((), ()))
    gate = lax.dot_general(x, w[:, :D], dims, preferred_element_type=jnp.float32)
    upper = lax.dot_general(x, w[:, D : 2 * D], dims, preferred_element_type=jnp.float32)
    inner = (gate / (1.0 + jnp.exp(-gate)) * upper).astype(jnp.bfloat16)
    out = jnp.dot(inner, w[:, 2 * D :], preferred_element_type=jnp.float32)
    o_ref[...] = out.astype(o_ref.dtype).reshape(o_ref.shape)


def experts(arrived, weights):
    groups, count, capacity, _ = arrived.shape
    hidden = weights.shape[1]
    return pl.pallas_call(
        ffn_kernel,
        out_shape=jax.ShapeDtypeStruct(arrived.shape, jnp.bfloat16),
        grid=(count,),
        in_specs=[
            pl.BlockSpec((groups, 1, capacity, D), lambda j: (0, j, 0, 0)),
            pl.BlockSpec((1, hidden, 3 * D), lambda j: (j, 0, 0)),
        ],
        out_specs=pl.BlockSpec((groups, 1, capacity, D), lambda j: (0, j, 0, 0)),
        compiler_params=pltpu.CompilerParams(
            dimension_semantics=("arbitrary",), vmem_limit_bytes=48 * 1024 * 1024
        ),
    )(arrived, weights)


def rms_scale(values, gain):
    floats = values.astype(jnp.float32)
    inverse = lax.rsqrt(jnp.mean(floats * floats, axis=-1, keepdims=True) + EPSILON)
    return (floats * inverse * gain).astype(jnp.bfloat16)


def rotate(values, positions):
    half_dim = values.shape[-1] // 2
    freqs = jnp.power(10000.0, -jnp.arange(half_dim, dtype=jnp.float32) / half_dim)
    angles = positions.astype(jnp.float32)[:, None] * freqs[None, :]
    cosine = jnp.cos(angles)[:, None, :]
    sine = jnp.sin(angles)[:, None, :]
    first = values[..., :half_dim]
    second = values[..., half_dim:]
    return jnp.concatenate(
        [first * cosine - second * sine, second * cosine + first * sine], axis=-1
    )


def local(
    hidden_states,
    attn_gain,
    w_qkv,
    w_out,
    kv_cache,
    cached_len,
    ffn_gain,
    w_router,
    expert_ids,
    w_gate,
    w_up,
    w_down,
):
    groups = HEADS // KVH
    tok_rows = hidden_states.shape[0]
    shard_pos = lax.axis_index("shard")
    length = cached_len[0]
    normed = rms_scale(hidden_states, attn_gain)
    qkv = jnp.dot(normed, w_qkv, preferred_element_type=jnp.float32)
    positions = length + shard_pos * tok_rows + jnp.arange(tok_rows, dtype=jnp.int32)
    queries = rotate(qkv[:, : HEADS * HD].reshape(tok_rows, HEADS, HD), positions).astype(
        jnp.bfloat16
    )
    new_keys = rotate(
        qkv[:, HEADS * HD : (HEADS + KVH) * HD].reshape(tok_rows, KVH, HD), positions
    ).astype(jnp.bfloat16)
    new_values = qkv[:, (HEADS + KVH) * HD :].astype(jnp.bfloat16)
    new_kv = jnp.concatenate([new_keys.reshape(tok_rows, KVH * HD), new_values], axis=1)
    cache = lax.all_gather(kv_cache[0], "shard", axis=0, tiled=True)
    shards = lax.axis_size("shard")
    fresh = [new_kv]
    for k in range(1, shards):
        pairs = [(s, s + k) for s in range(shards - k)]
        fresh.append(lax.ppermute(new_kv, "shard", pairs))
    fresh = jnp.concatenate(fresh, axis=0)
    query_rows = queries.reshape(tok_rows, KVH, groups, HD).transpose(1, 2, 0, 3)
    query_rows = query_rows.reshape(KVH, groups * tok_rows, HD)
    attended = attention(query_rows, cache, fresh, length, shard_pos * tok_rows)
    attended = attended.reshape(KVH, groups, tok_rows, HD).transpose(2, 0, 1, 3)
    attended = attended.reshape(tok_rows, HEADS * HD)
    mid = (
        hidden_states.astype(jnp.float32)
        + jnp.dot(attended, w_out, preferred_element_type=jnp.float32)
    ).astype(jnp.bfloat16)
    normed2 = rms_scale(mid, ffn_gain)
    group_count = lax.axis_size("req")
    local_experts = w_gate.shape[0]
    expert_count = local_experts * group_count
    capacity = min(tok_rows, 5 * tok_rows * TOP // (4 * expert_count))
    logits = jnp.dot(normed2, w_router, preferred_element_type=jnp.float32)
    picked = expert_ids[:, :, None] == jnp.arange(expert_count, dtype=jnp.int32)[None, None, :]
    chosen = jnp.sum(jnp.where(picked, logits[:, None, :], 0.0), axis=-1)
    gates = jax.nn.softmax(chosen, axis=-1)
    flat_hot = picked.reshape(tok_rows * TOP, expert_count).astype(jnp.int32)
    ranks = jnp.cumsum(flat_hot, axis=0) - flat_hot
    slot_rank = jnp.sum(ranks * flat_hot, axis=-1)
    slots = expert_ids.reshape(-1) * capacity + slot_rank
    slot_table = (
        slots.reshape(tok_rows, TOP)[:, :, None]
        == jnp.arange(expert_count * capacity, dtype=jnp.int32)[None, None, :]
    )
    placing = jnp.any(slot_table, axis=1).astype(jnp.bfloat16)
    outgoing = jnp.einsum("ts,td->sd", placing, normed2, preferred_element_type=jnp.float32).astype(
        jnp.bfloat16
    )
    outgoing = outgoing.reshape(group_count, local_experts, capacity, D)
    arrived = lax.all_to_all(outgoing, "req", split_axis=0, concat_axis=0, tiled=True)
    token_of = jnp.repeat(jnp.arange(tok_rows, dtype=jnp.float32), TOP)
    tags = jnp.zeros((expert_count * capacity, 2), jnp.float32)
    tags = tags.at[:, 0].set(-1.0).at[slots].set(jnp.stack([token_of, gates.reshape(-1)], axis=-1))
    tags = tags.reshape(group_count, local_experts * capacity, 2)
    tags = lax.all_to_all(tags, "req", split_axis=0, concat_axis=0, tiled=True)
    weights = jnp.concatenate([w_gate, w_up, w_down], axis=-1)
    weights = lax.all_gather(weights, "shard", axis=1, tiled=True)
    expert_rows = experts(arrived, weights).astype(jnp.float32)
    expert_rows = expert_rows.reshape(group_count, local_experts * capacity, D)
    owner = tags[..., 0].astype(jnp.int32)
    weighting = jnp.where(
        owner[:, None, :] == jnp.arange(tok_rows, dtype=jnp.int32)[None, :, None], tags[:, None, :, 1], 0.0
    )
    partial = jnp.einsum(
        "stm,smd->std", weighting, expert_rows, preferred_element_type=jnp.float32,
        precision=lax.Precision.HIGHEST,
    )
    returned = lax.all_to_all(partial.astype(jnp.bfloat16), "req", split_axis=0, concat_axis=0, tiled=True)
    mixture = jnp.sum(returned.astype(jnp.float32), axis=0)
    return (mid.astype(jnp.float32) + mixture).astype(jnp.bfloat16)


def solution(mesh):
    return jax.shard_map(
        local,
        mesh=mesh,
        in_specs=(
            P(("req", "shard"), None),
            P(),
            P(),
            P(),
            P("req", "shard", None),
            P("req"),
            P(),
            P(),
            P(("req", "shard"), None),
            P("req", "shard", None),
            P("req", "shard", None),
            P("req", "shard", None),
        ),
        out_specs=P(("req", "shard"), None),
        check_vma=False,
    )
```

```python
import functools
import math

import jax
import jax.numpy as jnp
from jax import lax
from jax.experimental import pallas as pl
from jax.experimental.pallas import tpu as pltpu
from jax.sharding import PartitionSpec as P

D = 1536
HEADS = 24
KVH = 8
HD = 64
TOP = 8


EPSILON = 1e-05
NEG_FILL = -1e30
FAR_LIMIT = 1 << 30
BLK = 512
NEG = NEG_FILL

def attn_kernel(meta_ref, q_ref, cache_ref, new_ref, o_ref, m_sc, l_sc, acc_sc, *, shards, rows):
    i = pl.program_id(0)
    length = meta_ref[0]
    own = meta_ref[1]
    tok = rows // (HEADS // KVH)
    chunk = cache_ref.shape[1]

    @pl.when(i == 0)
    def _():
        m_sc[...] = jnp.full(m_sc.shape, NEG, jnp.float32)
        l_sc[...] = jnp.zeros(l_sc.shape, jnp.float32)
        acc_sc[...] = jnp.zeros(acc_sc.shape, jnp.float32)

    def step(kv_ref, allowed):
        for g in range(KVH):
            q = q_ref[g]
            k = kv_ref[0, :, g * HD:(g + 1) * HD]
            v = kv_ref[0, :, KVH * HD + g * HD:KVH * HD + (g + 1) * HD]
            s = lax.dot_general(q, k, (((1,), (1,)), ((), ())), preferred_element_type=jnp.float32) * (HD ** -0.5)
            s = jnp.where(allowed, s, NEG)
            m_prev = m_sc[g]
            m_new = jnp.maximum(m_prev, jnp.max(s, axis=-1, keepdims=True))
            p = jnp.where(allowed, jnp.exp(s - m_new), 0.0)
            factor = jnp.exp(m_prev - m_new)
            l_sc[g] = l_sc[g] * factor + jnp.sum(p, axis=-1, keepdims=True)
            acc_sc[g] = acc_sc[g] * factor + jnp.dot(p.astype(jnp.bfloat16), v, preferred_element_type=jnp.float32)
            m_sc[g] = m_new

    @pl.when((i < shards) & (i * chunk < length))
    def _():
        key = i * chunk + lax.broadcasted_iota(jnp.int32, (rows, chunk), 1)
        step(cache_ref, key < length)

    j = i - shards

    @pl.when((i >= shards) & (j <= own))
    def _():
        key = j * tok + lax.broadcasted_iota(jnp.int32, (rows, tok), 1)
        qpos = own * tok + lax.broadcasted_iota(jnp.int32, (rows, tok), 0) % tok
        step(new_ref, key <= qpos)

    @pl.when(i == pl.num_programs(0) - 1)
    def _():
        for g in range(KVH):
            o_ref[g] = (acc_sc[g] / l_sc[g]).astype(o_ref.dtype)


def attention(queries, kv_all, length, own, chunk):
    shards = kv_all.shape[0]
    rows = queries.shape[1]
    tok = kv_all.shape[1] - chunk
    meta = jnp.stack([length, own]).astype(jnp.int32)
    kern = functools.partial(attn_kernel, shards=shards, rows=rows)
    width = kv_all.shape[2]
    return pl.pallas_call(
        kern,
        out_shape=jax.ShapeDtypeStruct((KVH, rows, HD), jnp.bfloat16),
        grid_spec=pltpu.PrefetchScalarGridSpec(
            num_scalar_prefetch=1,
            grid=(2 * shards,),
            in_specs=[
                pl.BlockSpec((KVH, rows, HD), lambda i, m: (0, 0, 0)),
                pl.BlockSpec((1, chunk, width), lambda i, m: (jnp.minimum(i, shards - 1), 0, 0)),
                pl.BlockSpec(
                    (1, tok, width), lambda i, m: (jnp.maximum(i - shards, 0), chunk // tok, 0)
                ),
            ],
            out_specs=pl.BlockSpec((KVH, rows, HD), lambda i, m: (0, 0, 0)),
            scratch_shapes=[
                pltpu.VMEM((KVH, rows, 1), jnp.float32),
                pltpu.VMEM((KVH, rows, 1), jnp.float32),
                pltpu.VMEM((KVH, rows, HD), jnp.float32),
            ],
        ),
        compiler_params=pltpu.CompilerParams(dimension_semantics=("arbitrary",)),
    )(meta, queries, kv_all, kv_all)

def ffn_kernel(x_ref, w_ref, o_ref):
    rows = x_ref.shape[0] * x_ref.shape[2]
    x = x_ref[...].reshape(rows, D)
    w = w_ref[0]
    dims = (((1,), (1,)), ((), ()))
    gate = lax.dot_general(x, w[:, :D], dims, preferred_element_type=jnp.float32)
    upper = lax.dot_general(x, w[:, D : 2 * D], dims, preferred_element_type=jnp.float32)
    inner = (gate / (1.0 + jnp.exp(-gate)) * upper).astype(jnp.bfloat16)
    out = jnp.dot(inner, w[:, 2 * D :], preferred_element_type=jnp.float32)
    o_ref[...] = out.astype(o_ref.dtype).reshape(o_ref.shape)


def experts(arrived, weights):
    groups, count, capacity, _ = arrived.shape
    hidden = weights.shape[1]
    return pl.pallas_call(
        ffn_kernel,
        out_shape=jax.ShapeDtypeStruct(arrived.shape, jnp.bfloat16),
        grid=(count,),
        in_specs=[
            pl.BlockSpec((groups, 1, capacity, D), lambda j: (0, j, 0, 0)),
            pl.BlockSpec((1, hidden, 3 * D), lambda j: (j, 0, 0)),
        ],
        out_specs=pl.BlockSpec((groups, 1, capacity, D), lambda j: (0, j, 0, 0)),
        compiler_params=pltpu.CompilerParams(
            dimension_semantics=("arbitrary",), vmem_limit_bytes=48 * 1024 * 1024
        ),
    )(arrived, weights)


def rms_scale(values, gain):
    floats = values.astype(jnp.float32)
    inverse = lax.rsqrt(jnp.mean(floats * floats, axis=-1, keepdims=True) + EPSILON)
    return (floats * inverse * gain).astype(jnp.bfloat16)


def rotate(values, positions):
    half_dim = values.shape[-1] // 2
    freqs = jnp.power(10000.0, -jnp.arange(half_dim, dtype=jnp.float32) / half_dim)
    angles = positions.astype(jnp.float32)[:, None] * freqs[None, :]
    cosine = jnp.cos(angles)[:, None, :]
    sine = jnp.sin(angles)[:, None, :]
    first = values[..., :half_dim]
    second = values[..., half_dim:]
    return jnp.concatenate(
        [first * cosine - second * sine, second * cosine + first * sine], axis=-1
    )


def local(
    hidden_states,
    attn_gain,
    w_qkv,
    w_out,
    kv_cache,
    cached_len,
    ffn_gain,
    w_router,
    expert_ids,
    w_gate,
    w_up,
    w_down,
):
    groups = HEADS // KVH
    tok_rows = hidden_states.shape[0]
    shard_pos = lax.axis_index("shard")
    length = cached_len[0]
    normed = rms_scale(hidden_states, attn_gain)
    qkv = jnp.dot(normed, w_qkv, preferred_element_type=jnp.float32)
    positions = length + shard_pos * tok_rows + jnp.arange(tok_rows, dtype=jnp.int32)
    queries = rotate(qkv[:, : HEADS * HD].reshape(tok_rows, HEADS, HD), positions).astype(
        jnp.bfloat16
    )
    new_keys = rotate(
        qkv[:, HEADS * HD : (HEADS + KVH) * HD].reshape(tok_rows, KVH, HD), positions
    ).astype(jnp.bfloat16)
    new_values = qkv[:, (HEADS + KVH) * HD :].astype(jnp.bfloat16)
    new_kv = jnp.concatenate([new_keys.reshape(tok_rows, KVH * HD), new_values], axis=1)
    joined = jnp.concatenate([kv_cache[0], new_kv], axis=0)
    kv_all = lax.all_gather(joined, "shard", axis=0, tiled=False)
    query_rows = queries.reshape(tok_rows, KVH, groups, HD).transpose(1, 2, 0, 3)
    query_rows = query_rows.reshape(KVH, groups * tok_rows, HD)
    attended = attention(query_rows, kv_all, length, shard_pos, kv_cache.shape[1])
    attended = attended.reshape(KVH, groups, tok_rows, HD).transpose(2, 0, 1, 3)
    attended = attended.reshape(tok_rows, HEADS * HD)
    mid = (
        hidden_states.astype(jnp.float32)
        + jnp.dot(attended, w_out, preferred_element_type=jnp.float32)
    ).astype(jnp.bfloat16)
    normed2 = rms_scale(mid, ffn_gain)
    group_count = lax.axis_size("req")
    local_experts = w_gate.shape[0]
    expert_count = local_experts * group_count
    capacity = min(tok_rows, 5 * tok_rows * TOP // (4 * expert_count))
    logits = jnp.dot(normed2, w_router, preferred_element_type=jnp.float32)
    picked = expert_ids[:, :, None] == jnp.arange(expert_count, dtype=jnp.int32)[None, None, :]
    chosen = jnp.sum(jnp.where(picked, logits[:, None, :], 0.0), axis=-1)
    gates = jax.nn.softmax(chosen, axis=-1)
    flat_hot = picked.reshape(tok_rows * TOP, expert_count).astype(jnp.int32)
    ranks = jnp.cumsum(flat_hot, axis=0) - flat_hot
    slot_rank = jnp.sum(ranks * flat_hot, axis=-1)
    slots = expert_ids.reshape(-1) * capacity + slot_rank
    slot_table = (
        slots.reshape(tok_rows, TOP)[:, :, None]
        == jnp.arange(expert_count * capacity, dtype=jnp.int32)[None, None, :]
    )
    placing = jnp.any(slot_table, axis=1).astype(jnp.bfloat16)
    outgoing = jnp.einsum("ts,td->sd", placing, normed2, preferred_element_type=jnp.float32).astype(
        jnp.bfloat16
    )
    outgoing = outgoing.reshape(group_count, local_experts, capacity, D)
    arrived = lax.all_to_all(outgoing, "req", split_axis=0, concat_axis=0, tiled=True)
    token_of = jnp.repeat(jnp.arange(tok_rows, dtype=jnp.float32), TOP)
    tags = jnp.zeros((expert_count * capacity, 2), jnp.float32)
    tags = tags.at[:, 0].set(-1.0).at[slots].set(jnp.stack([token_of, gates.reshape(-1)], axis=-1))
    tags = tags.reshape(group_count, local_experts * capacity, 2)
    tags = lax.all_to_all(tags, "req", split_axis=0, concat_axis=0, tiled=True)
    weights = jnp.concatenate([w_gate, w_up, w_down], axis=-1)
    weights = lax.all_gather(weights, "shard", axis=1, tiled=True)
    expert_rows = experts(arrived, weights).astype(jnp.float32)
    expert_rows = expert_rows.reshape(group_count, local_experts * capacity, D)
    owner = tags[..., 0].astype(jnp.int32)
    weighting = jnp.where(
        owner[:, None, :] == jnp.arange(tok_rows, dtype=jnp.int32)[None, :, None], tags[:, None, :, 1], 0.0
    )
    partial = jnp.einsum(
        "stm,smd->std", weighting, expert_rows, preferred_element_type=jnp.float32,
        precision=lax.Precision.HIGHEST,
    )
    returned = lax.all_to_all(partial.astype(jnp.bfloat16), "req", split_axis=0, concat_axis=0, tiled=True)
    mixture = jnp.sum(returned.astype(jnp.float32), axis=0)
    return (mid.astype(jnp.float32) + mixture).astype(jnp.bfloat16)


def solution(mesh):
    return jax.shard_map(
        local,
        mesh=mesh,
        in_specs=(
            P(("req", "shard"), None),
            P(),
            P(),
            P(),
            P("req", "shard", None),
            P("req"),
            P(),
            P(),
            P(("req", "shard"), None),
            P("req", "shard", None),
            P("req", "shard", None),
            P("req", "shard", None),
        ),
        out_specs=P(("req", "shard"), None),
        check_vma=False,
    )
```

```python
import functools
import math

import jax
import jax.numpy as jnp
from jax import lax
from jax.experimental import pallas as pl
from jax.experimental.pallas import tpu as pltpu
from jax.sharding import PartitionSpec as P

D = 1536
HEADS = 24
KVH = 8
HD = 64
TOP = 8


EPSILON = 1e-05
NEG_FILL = -1e30
FAR_LIMIT = 1 << 30
BLK = 512
NEG = NEG_FILL

def attn_kernel(meta_ref, q_ref, cache_ref, new_ref, o_ref, m_sc, l_sc, acc_sc, *, n_cache, rows):
    i = pl.program_id(0)
    length = meta_ref[0]
    qbase = meta_ref[1]

    @pl.when(i == 0)
    def _():
        m_sc[...] = jnp.full(m_sc.shape, NEG, jnp.float32)
        l_sc[...] = jnp.zeros(l_sc.shape, jnp.float32)
        acc_sc[...] = jnp.zeros(acc_sc.shape, jnp.float32)

    def step(kv_ref, allowed):
        parts = kv_ref.shape[0]
        for g in range(KVH):
            q = q_ref[g]
            k = jnp.concatenate([kv_ref[c, :, g * HD:(g + 1) * HD] for c in range(parts)], axis=0)
            v = jnp.concatenate(
                [kv_ref[c, :, KVH * HD + g * HD:KVH * HD + (g + 1) * HD] for c in range(parts)], axis=0
            )
            s = lax.dot_general(q, k, (((1,), (1,)), ((), ())), preferred_element_type=jnp.float32) * (HD ** -0.5)
            s = jnp.where(allowed, s, NEG)
            m_prev = m_sc[g]
            m_new = jnp.maximum(m_prev, jnp.max(s, axis=-1, keepdims=True))
            p = jnp.where(allowed, jnp.exp(s - m_new), 0.0)
            factor = jnp.exp(m_prev - m_new)
            l_sc[g] = l_sc[g] * factor + jnp.sum(p, axis=-1, keepdims=True)
            acc_sc[g] = acc_sc[g] * factor + jnp.dot(p.astype(jnp.bfloat16), v, preferred_element_type=jnp.float32)
            m_sc[g] = m_new

    @pl.when((i < n_cache) & (i * BLK < length))
    def _():
        key = i * BLK + lax.broadcasted_iota(jnp.int32, (rows, BLK), 1)
        step(cache_ref, key < length)

    j = i - n_cache
    tok = rows // (HEADS // KVH)

    @pl.when((i >= n_cache) & (j * BLK <= qbase + tok - 1))
    def _():
        key = j * BLK + lax.broadcasted_iota(jnp.int32, (rows, BLK), 1)
        qpos = qbase + lax.broadcasted_iota(jnp.int32, (rows, BLK), 0) % tok
        step(new_ref, key <= qpos)

    @pl.when(i == pl.num_programs(0) - 1)
    def _():
        for g in range(KVH):
            o_ref[g] = (acc_sc[g] / l_sc[g]).astype(o_ref.dtype)


def attention(queries, kv_all, length, qbase, chunk):
    shards, _, width = kv_all.shape
    rows = queries.shape[1]
    tok = kv_all.shape[1] - chunk
    cache_parts = BLK // chunk
    new_parts = BLK // tok
    n_cache = shards // cache_parts
    n_new = shards // new_parts
    meta = jnp.stack([length, qbase]).astype(jnp.int32)
    kern = functools.partial(attn_kernel, n_cache=n_cache, rows=rows)
    return pl.pallas_call(
        kern,
        out_shape=jax.ShapeDtypeStruct((KVH, rows, HD), jnp.bfloat16),
        grid_spec=pltpu.PrefetchScalarGridSpec(
            num_scalar_prefetch=1,
            grid=(n_cache + n_new,),
            in_specs=[
                pl.BlockSpec((KVH, rows, HD), lambda i, m: (0, 0, 0)),
                pl.BlockSpec(
                    (cache_parts, chunk, width), lambda i, m: (jnp.minimum(i, n_cache - 1), 0, 0)
                ),
                pl.BlockSpec(
                    (new_parts, tok, width), lambda i, m: (jnp.maximum(i - n_cache, 0), chunk // tok, 0)
                ),
            ],
            out_specs=pl.BlockSpec((KVH, rows, HD), lambda i, m: (0, 0, 0)),
            scratch_shapes=[
                pltpu.VMEM((KVH, rows, 1), jnp.float32),
                pltpu.VMEM((KVH, rows, 1), jnp.float32),
                pltpu.VMEM((KVH, rows, HD), jnp.float32),
            ],
        ),
        compiler_params=pltpu.CompilerParams(dimension_semantics=("arbitrary",)),
    )(meta, queries, kv_all, kv_all)

def ffn_kernel(x_ref, w_ref, o_ref):
    rows = x_ref.shape[0] * x_ref.shape[2]
    x = x_ref[...].reshape(rows, D)
    w = w_ref[0]
    dims = (((1,), (1,)), ((), ()))
    gate = lax.dot_general(x, w[:, :D], dims, preferred_element_type=jnp.float32)
    upper = lax.dot_general(x, w[:, D : 2 * D], dims, preferred_element_type=jnp.float32)
    inner = (gate / (1.0 + jnp.exp(-gate)) * upper).astype(jnp.bfloat16)
    out = jnp.dot(inner, w[:, 2 * D :], preferred_element_type=jnp.float32)
    o_ref[...] = out.astype(o_ref.dtype).reshape(o_ref.shape)


def experts(arrived, weights):
    groups, count, capacity, _ = arrived.shape
    hidden = weights.shape[1]
    return pl.pallas_call(
        ffn_kernel,
        out_shape=jax.ShapeDtypeStruct(arrived.shape, jnp.bfloat16),
        grid=(count,),
        in_specs=[
            pl.BlockSpec((groups, 1, capacity, D), lambda j: (0, j, 0, 0)),
            pl.BlockSpec((1, hidden, 3 * D), lambda j: (j, 0, 0)),
        ],
        out_specs=pl.BlockSpec((groups, 1, capacity, D), lambda j: (0, j, 0, 0)),
        compiler_params=pltpu.CompilerParams(
            dimension_semantics=("arbitrary",), vmem_limit_bytes=48 * 1024 * 1024
        ),
    )(arrived, weights)


def rms_scale(values, gain):
    floats = values.astype(jnp.float32)
    inverse = lax.rsqrt(jnp.mean(floats * floats, axis=-1, keepdims=True) + EPSILON)
    return (floats * inverse * gain).astype(jnp.bfloat16)


def rotate(values, positions):
    half_dim = values.shape[-1] // 2
    freqs = jnp.power(10000.0, -jnp.arange(half_dim, dtype=jnp.float32) / half_dim)
    angles = positions.astype(jnp.float32)[:, None] * freqs[None, :]
    cosine = jnp.cos(angles)[:, None, :]
    sine = jnp.sin(angles)[:, None, :]
    first = values[..., :half_dim]
    second = values[..., half_dim:]
    return jnp.concatenate(
        [first * cosine - second * sine, second * cosine + first * sine], axis=-1
    )


def local(
    hidden_states,
    attn_gain,
    w_qkv,
    w_out,
    kv_cache,
    cached_len,
    ffn_gain,
    w_router,
    expert_ids,
    w_gate,
    w_up,
    w_down,
):
    groups = HEADS // KVH
    tok_rows = hidden_states.shape[0]
    shard_pos = lax.axis_index("shard")
    length = cached_len[0]
    normed = rms_scale(hidden_states, attn_gain)
    qkv = jnp.dot(normed, w_qkv, preferred_element_type=jnp.float32)
    positions = length + shard_pos * tok_rows + jnp.arange(tok_rows, dtype=jnp.int32)
    queries = rotate(qkv[:, : HEADS * HD].reshape(tok_rows, HEADS, HD), positions).astype(
        jnp.bfloat16
    )
    new_keys = rotate(
        qkv[:, HEADS * HD : (HEADS + KVH) * HD].reshape(tok_rows, KVH, HD), positions
    ).astype(jnp.bfloat16)
    new_values = qkv[:, (HEADS + KVH) * HD :].astype(jnp.bfloat16)
    new_kv = jnp.concatenate([new_keys.reshape(tok_rows, KVH * HD), new_values], axis=1)
    joined = jnp.concatenate([kv_cache[0], new_kv], axis=0)
    kv_all = lax.all_gather(joined, "shard", axis=0, tiled=False)
    query_rows = queries.reshape(tok_rows, KVH, groups, HD).transpose(1, 2, 0, 3)
    query_rows = query_rows.reshape(KVH, groups * tok_rows, HD)
    attended = attention(query_rows, kv_all, length, shard_pos * tok_rows, kv_cache.shape[1])
    attended = attended.reshape(KVH, groups, tok_rows, HD).transpose(2, 0, 1, 3)
    attended = attended.reshape(tok_rows, HEADS * HD)
    mid = (
        hidden_states.astype(jnp.float32)
        + jnp.dot(attended, w_out, preferred_element_type=jnp.float32)
    ).astype(jnp.bfloat16)
    normed2 = rms_scale(mid, ffn_gain)
    group_count = lax.axis_size("req")
    local_experts = w_gate.shape[0]
    expert_count = local_experts * group_count
    capacity = min(tok_rows, 5 * tok_rows * TOP // (4 * expert_count))
    logits = jnp.dot(normed2, w_router, preferred_element_type=jnp.float32)
    picked = expert_ids[:, :, None] == jnp.arange(expert_count, dtype=jnp.int32)[None, None, :]
    chosen = jnp.sum(jnp.where(picked, logits[:, None, :], 0.0), axis=-1)
    gates = jax.nn.softmax(chosen, axis=-1)
    flat_hot = picked.reshape(tok_rows * TOP, expert_count).astype(jnp.int32)
    ranks = jnp.cumsum(flat_hot, axis=0) - flat_hot
    slot_rank = jnp.sum(ranks * flat_hot, axis=-1)
    slots = expert_ids.reshape(-1) * capacity + slot_rank
    slot_table = (
        slots.reshape(tok_rows, TOP)[:, :, None]
        == jnp.arange(expert_count * capacity, dtype=jnp.int32)[None, None, :]
    )
    placing = jnp.any(slot_table, axis=1).astype(jnp.bfloat16)
    outgoing = jnp.einsum("ts,td->sd", placing, normed2, preferred_element_type=jnp.float32).astype(
        jnp.bfloat16
    )
    outgoing = outgoing.reshape(group_count, local_experts, capacity, D)
    arrived = lax.all_to_all(outgoing, "req", split_axis=0, concat_axis=0, tiled=True)
    token_of = jnp.repeat(jnp.arange(tok_rows, dtype=jnp.float32), TOP)
    tags = jnp.zeros((expert_count * capacity, 2), jnp.float32)
    tags = tags.at[:, 0].set(-1.0).at[slots].set(jnp.stack([token_of, gates.reshape(-1)], axis=-1))
    tags = tags.reshape(group_count, local_experts * capacity, 2)
    tags = lax.all_to_all(tags, "req", split_axis=0, concat_axis=0, tiled=True)
    weights = jnp.concatenate([w_gate, w_up, w_down], axis=-1)
    weights = lax.all_gather(weights, "shard", axis=1, tiled=True)
    expert_rows = experts(arrived, weights).astype(jnp.float32)
    expert_rows = expert_rows.reshape(group_count, local_experts * capacity, D)
    owner = tags[..., 0].astype(jnp.int32)
    weighting = jnp.where(
        owner[:, None, :] == jnp.arange(tok_rows, dtype=jnp.int32)[None, :, None], tags[:, None, :, 1], 0.0
    )
    partial = jnp.einsum(
        "stm,smd->std", weighting, expert_rows, preferred_element_type=jnp.float32,
        precision=lax.Precision.HIGHEST,
    )
    returned = lax.all_to_all(partial.astype(jnp.bfloat16), "req", split_axis=0, concat_axis=0, tiled=True)
    mixture = jnp.sum(returned.astype(jnp.float32), axis=0)
    return (mid.astype(jnp.float32) + mixture).astype(jnp.bfloat16)


def solution(mesh):
    return jax.shard_map(
        local,
        mesh=mesh,
        in_specs=(
            P(("req", "shard"), None),
            P(),
            P(),
            P(),
            P("req", "shard", None),
            P("req"),
            P(),
            P(),
            P(("req", "shard"), None),
            P("req", "shard", None),
            P("req", "shard", None),
            P("req", "shard", None),
        ),
        out_specs=P(("req", "shard"), None),
        check_vma=False,
    )
```

```python
import functools
import math

import jax
import jax.numpy as jnp
from jax import lax
from jax.experimental import pallas as pl
from jax.experimental.pallas import tpu as pltpu
from jax.sharding import PartitionSpec as P

D = 1536
HEADS = 24
KVH = 8
HD = 64
TOP = 8


EPSILON = 1e-05
NEG_FILL = -1e30
FAR_LIMIT = 1 << 30
BLK = 512
NEG = NEG_FILL

def attn_kernel(meta_ref, q_ref, cache_ref, new_ref, o_ref, m_sc, l_sc, acc_sc, *, n_cache, rows):
    i = pl.program_id(0)
    length = meta_ref[0]
    qbase = meta_ref[1]

    @pl.when(i == 0)
    def _():
        m_sc[...] = jnp.full(m_sc.shape, NEG, jnp.float32)
        l_sc[...] = jnp.zeros(l_sc.shape, jnp.float32)
        acc_sc[...] = jnp.zeros(acc_sc.shape, jnp.float32)

    def step(kv_ref, allowed):
        parts = kv_ref.shape[0]
        for g in range(KVH):
            q = q_ref[g]
            k = jnp.concatenate([kv_ref[c, :, g * HD:(g + 1) * HD] for c in range(parts)], axis=0)
            v = jnp.concatenate(
                [kv_ref[c, :, KVH * HD + g * HD:KVH * HD + (g + 1) * HD] for c in range(parts)], axis=0
            )
            s = lax.dot_general(q, k, (((1,), (1,)), ((), ())), preferred_element_type=jnp.float32) * (HD ** -0.5)
            s = jnp.where(allowed, s, NEG)
            m_prev = m_sc[g]
            m_new = jnp.maximum(m_prev, jnp.max(s, axis=-1, keepdims=True))
            p = jnp.where(allowed, jnp.exp(s - m_new), 0.0)
            factor = jnp.exp(m_prev - m_new)
            l_sc[g] = l_sc[g] * factor + jnp.sum(p, axis=-1, keepdims=True)
            acc_sc[g] = acc_sc[g] * factor + jnp.dot(p.astype(jnp.bfloat16), v, preferred_element_type=jnp.float32)
            m_sc[g] = m_new

    @pl.when((i < n_cache) & (i * BLK < length))
    def _():
        key = i * BLK + lax.broadcasted_iota(jnp.int32, (rows, BLK), 1)
        step(cache_ref, key < length)

    j = i - n_cache
    tok = rows // (HEADS // KVH)

    @pl.when((i >= n_cache) & (j * BLK <= qbase + tok - 1))
    def _():
        key = j * BLK + lax.broadcasted_iota(jnp.int32, (rows, BLK), 1)
        qpos = qbase + lax.broadcasted_iota(jnp.int32, (rows, BLK), 0) % tok
        step(new_ref, key <= qpos)

    @pl.when(i == pl.num_programs(0) - 1)
    def _():
        for g in range(KVH):
            o_ref[g] = (acc_sc[g] / l_sc[g]).astype(o_ref.dtype)


def attention(queries, kv_all, length, qbase, chunk):
    shards, _, width = kv_all.shape
    rows = queries.shape[1]
    tok = kv_all.shape[1] - chunk
    cache_parts = BLK // chunk
    new_parts = BLK // tok
    n_cache = shards // cache_parts
    n_new = shards // new_parts
    meta = jnp.stack([length, qbase]).astype(jnp.int32)
    kern = functools.partial(attn_kernel, n_cache=n_cache, rows=rows)
    return pl.pallas_call(
        kern,
        out_shape=jax.ShapeDtypeStruct((KVH, rows, HD), jnp.bfloat16),
        grid_spec=pltpu.PrefetchScalarGridSpec(
            num_scalar_prefetch=1,
            grid=(n_cache + n_new,),
            in_specs=[
                pl.BlockSpec((KVH, rows, HD), lambda i, m: (0, 0, 0)),
                pl.BlockSpec(
                    (cache_parts, chunk, width), lambda i, m: (jnp.minimum(i, n_cache - 1), 0, 0)
                ),
                pl.BlockSpec(
                    (new_parts, tok, width), lambda i, m: (jnp.maximum(i - n_cache, 0), chunk // tok, 0)
                ),
            ],
            out_specs=pl.BlockSpec((KVH, rows, HD), lambda i, m: (0, 0, 0)),
            scratch_shapes=[
                pltpu.VMEM((KVH, rows, 1), jnp.float32),
                pltpu.VMEM((KVH, rows, 1), jnp.float32),
                pltpu.VMEM((KVH, rows, HD), jnp.float32),
            ],
        ),
        compiler_params=pltpu.CompilerParams(dimension_semantics=("arbitrary",)),
    )(meta, queries, kv_all, kv_all)

def ffn_kernel(x_ref, w_ref, g_ref, o_ref, acc_ref):
    j = pl.program_id(0)
    groups, _, capacity, _ = x_ref.shape
    rows = groups * capacity
    x = x_ref[...].reshape(rows, D)
    w = w_ref[0]
    dims = (((1,), (1,)), ((), ()))
    gate = lax.dot_general(x, w[:, :D], dims, preferred_element_type=jnp.float32)
    upper = lax.dot_general(x, w[:, D : 2 * D], dims, preferred_element_type=jnp.float32)
    inner = (gate / (1.0 + jnp.exp(-gate)) * upper).astype(jnp.bfloat16)
    out = jnp.dot(inner, w[:, 2 * D :], preferred_element_type=jnp.float32).astype(jnp.bfloat16)

    @pl.when(j == 0)
    def _():
        acc_ref[...] = jnp.zeros(acc_ref.shape, jnp.float32)

    for s in range(groups):
        share = g_ref[0, s]
        high = share.astype(jnp.bfloat16)
        low = (share - high.astype(jnp.float32)).astype(jnp.bfloat16)
        rows_s = out[s * capacity : (s + 1) * capacity]
        acc_ref[s] += jnp.dot(high, rows_s, preferred_element_type=jnp.float32) + jnp.dot(
            low, rows_s, preferred_element_type=jnp.float32
        )

    @pl.when(j == pl.num_programs(0) - 1)
    def _():
        o_ref[...] = acc_ref[...].astype(o_ref.dtype)


def experts(arrived, weights, shares):
    groups, count, capacity, _ = arrived.shape
    hidden = weights.shape[1]
    tokens = shares.shape[2]
    return pl.pallas_call(
        ffn_kernel,
        out_shape=jax.ShapeDtypeStruct((groups, tokens, D), jnp.bfloat16),
        grid=(count,),
        in_specs=[
            pl.BlockSpec((groups, 1, capacity, D), lambda j: (0, j, 0, 0)),
            pl.BlockSpec((1, hidden, 3 * D), lambda j: (j, 0, 0)),
            pl.BlockSpec((1, groups, tokens, capacity), lambda j: (j, 0, 0, 0)),
        ],
        out_specs=pl.BlockSpec((groups, tokens, D), lambda j: (0, 0, 0)),
        scratch_shapes=[pltpu.VMEM((groups, tokens, D), jnp.float32)],
        compiler_params=pltpu.CompilerParams(
            dimension_semantics=("arbitrary",), vmem_limit_bytes=48 * 1024 * 1024
        ),
    )(arrived, weights, shares)

def rms_scale(values, gain):
    floats = values.astype(jnp.float32)
    inverse = lax.rsqrt(jnp.mean(floats * floats, axis=-1, keepdims=True) + EPSILON)
    return (floats * inverse * gain).astype(jnp.bfloat16)


def rotate(values, positions):
    half_dim = values.shape[-1] // 2
    freqs = jnp.power(10000.0, -jnp.arange(half_dim, dtype=jnp.float32) / half_dim)
    angles = positions.astype(jnp.float32)[:, None] * freqs[None, :]
    cosine = jnp.cos(angles)[:, None, :]
    sine = jnp.sin(angles)[:, None, :]
    first = values[..., :half_dim]
    second = values[..., half_dim:]
    return jnp.concatenate(
        [first * cosine - second * sine, second * cosine + first * sine], axis=-1
    )


def local(
    hidden_states,
    attn_gain,
    w_qkv,
    w_out,
    kv_cache,
    cached_len,
    ffn_gain,
    w_router,
    expert_ids,
    w_gate,
    w_up,
    w_down,
):
    groups = HEADS // KVH
    tok_rows = hidden_states.shape[0]
    shard_pos = lax.axis_index("shard")
    length = cached_len[0]
    normed = rms_scale(hidden_states, attn_gain)
    qkv = jnp.dot(normed, w_qkv, preferred_element_type=jnp.float32)
    positions = length + shard_pos * tok_rows + jnp.arange(tok_rows, dtype=jnp.int32)
    queries = rotate(qkv[:, : HEADS * HD].reshape(tok_rows, HEADS, HD), positions).astype(
        jnp.bfloat16
    )
    new_keys = rotate(
        qkv[:, HEADS * HD : (HEADS + KVH) * HD].reshape(tok_rows, KVH, HD), positions
    ).astype(jnp.bfloat16)
    new_values = qkv[:, (HEADS + KVH) * HD :].astype(jnp.bfloat16)
    new_kv = jnp.concatenate([new_keys.reshape(tok_rows, KVH * HD), new_values], axis=1)
    joined = jnp.concatenate([kv_cache[0], new_kv], axis=0)
    kv_all = lax.all_gather(joined, "shard", axis=0, tiled=False)
    query_rows = queries.reshape(tok_rows, KVH, groups, HD).transpose(1, 2, 0, 3)
    query_rows = query_rows.reshape(KVH, groups * tok_rows, HD)
    attended = attention(query_rows, kv_all, length, shard_pos * tok_rows, kv_cache.shape[1])
    attended = attended.reshape(KVH, groups, tok_rows, HD).transpose(2, 0, 1, 3)
    attended = attended.reshape(tok_rows, HEADS * HD)
    mid = (
        hidden_states.astype(jnp.float32)
        + jnp.dot(attended, w_out, preferred_element_type=jnp.float32)
    ).astype(jnp.bfloat16)
    normed2 = rms_scale(mid, ffn_gain)
    group_count = lax.axis_size("req")
    local_experts = w_gate.shape[0]
    expert_count = local_experts * group_count
    capacity = min(tok_rows, 5 * tok_rows * TOP // (4 * expert_count))
    logits = jnp.dot(normed2, w_router, preferred_element_type=jnp.float32)
    picked = expert_ids[:, :, None] == jnp.arange(expert_count, dtype=jnp.int32)[None, None, :]
    chosen = jnp.sum(jnp.where(picked, logits[:, None, :], 0.0), axis=-1)
    gates = jax.nn.softmax(chosen, axis=-1)
    flat_hot = picked.reshape(tok_rows * TOP, expert_count).astype(jnp.int32)
    ranks = jnp.cumsum(flat_hot, axis=0) - flat_hot
    slot_rank = jnp.sum(ranks * flat_hot, axis=-1)
    slots = expert_ids.reshape(-1) * capacity + slot_rank
    slot_table = (
        slots.reshape(tok_rows, TOP)[:, :, None]
        == jnp.arange(expert_count * capacity, dtype=jnp.int32)[None, None, :]
    )
    placing = jnp.any(slot_table, axis=1).astype(jnp.bfloat16)
    outgoing = jnp.einsum("ts,td->sd", placing, normed2, preferred_element_type=jnp.float32).astype(
        jnp.bfloat16
    )
    outgoing = outgoing.reshape(group_count, local_experts, capacity, D)
    arrived = lax.all_to_all(outgoing, "req", split_axis=0, concat_axis=0, tiled=True)
    token_of = jnp.repeat(jnp.arange(tok_rows, dtype=jnp.float32), TOP)
    tags = jnp.zeros((expert_count * capacity, 2), jnp.float32)
    tags = tags.at[:, 0].set(-1.0).at[slots].set(jnp.stack([token_of, gates.reshape(-1)], axis=-1))
    tags = tags.reshape(group_count, local_experts * capacity, 2)
    tags = lax.all_to_all(tags, "req", split_axis=0, concat_axis=0, tiled=True)
    weights = jnp.concatenate([w_gate, w_up, w_down], axis=-1)
    weights = lax.all_gather(weights, "shard", axis=1, tiled=True)
    owner = tags[..., 0].astype(jnp.int32)
    weighting = jnp.where(
        owner[:, None, :] == jnp.arange(tok_rows, dtype=jnp.int32)[None, :, None], tags[:, None, :, 1], 0.0
    )
    shares = weighting.reshape(group_count, tok_rows, local_experts, capacity).transpose(2, 0, 1, 3)
    partial = experts(arrived, weights, shares)
    returned = lax.all_to_all(partial, "req", split_axis=0, concat_axis=0, tiled=True)
    mixture = jnp.sum(returned.astype(jnp.float32), axis=0)
    return (mid.astype(jnp.float32) + mixture).astype(jnp.bfloat16)


def solution(mesh):
    return jax.shard_map(
        local,
        mesh=mesh,
        in_specs=(
            P(("req", "shard"), None),
            P(),
            P(),
            P(),
            P("req", "shard", None),
            P("req"),
            P(),
            P(),
            P(("req", "shard"), None),
            P("req", "shard", None),
            P("req", "shard", None),
            P("req", "shard", None),
        ),
        out_specs=P(("req", "shard"), None),
        check_vma=False,
    )
```

```python
import functools
import math

import jax
import jax.numpy as jnp
from jax import lax
from jax.experimental import pallas as pl
from jax.experimental.pallas import tpu as pltpu
from jax.sharding import PartitionSpec as P

D = 1536
HEADS = 24
KVH = 8
HD = 64
TOP = 8


EPSILON = 1e-05
NEG_FILL = -1e30
FAR_LIMIT = 1 << 30
BLK = 512
NEG = NEG_FILL

def attn_kernel(meta_ref, q_ref, cache_ref, new_ref, o_ref, m_sc, l_sc, acc_sc, *, n_cache, rows):
    i = pl.program_id(0)
    length = meta_ref[0]
    qbase = meta_ref[1]

    @pl.when(i == 0)
    def _():
        m_sc[...] = jnp.full(m_sc.shape, NEG, jnp.float32)
        l_sc[...] = jnp.zeros(l_sc.shape, jnp.float32)
        acc_sc[...] = jnp.zeros(acc_sc.shape, jnp.float32)

    def step(kv_ref, allowed):
        parts = kv_ref.shape[0]
        for g in range(KVH):
            q = q_ref[g]
            k = jnp.concatenate([kv_ref[c, :, g * HD:(g + 1) * HD] for c in range(parts)], axis=0)
            v = jnp.concatenate(
                [kv_ref[c, :, KVH * HD + g * HD:KVH * HD + (g + 1) * HD] for c in range(parts)], axis=0
            )
            s = lax.dot_general(q, k, (((1,), (1,)), ((), ())), preferred_element_type=jnp.float32) * (HD ** -0.5)
            s = jnp.where(allowed, s, NEG)
            m_prev = m_sc[g]
            m_new = jnp.maximum(m_prev, jnp.max(s, axis=-1, keepdims=True))
            p = jnp.where(allowed, jnp.exp(s - m_new), 0.0)
            factor = jnp.exp(m_prev - m_new)
            l_sc[g] = l_sc[g] * factor + jnp.sum(p, axis=-1, keepdims=True)
            acc_sc[g] = acc_sc[g] * factor + jnp.dot(p.astype(jnp.bfloat16), v, preferred_element_type=jnp.float32)
            m_sc[g] = m_new

    @pl.when((i < n_cache) & (i * BLK < length))
    def _():
        key = i * BLK + lax.broadcasted_iota(jnp.int32, (rows, BLK), 1)
        step(cache_ref, key < length)

    j = i - n_cache
    tok = rows // (HEADS // KVH)

    @pl.when((i >= n_cache) & (j * BLK <= qbase + tok - 1))
    def _():
        key = j * BLK + lax.broadcasted_iota(jnp.int32, (rows, BLK), 1)
        qpos = qbase + lax.broadcasted_iota(jnp.int32, (rows, BLK), 0) % tok
        step(new_ref, key <= qpos)

    @pl.when(i == pl.num_programs(0) - 1)
    def _():
        for g in range(KVH):
            o_ref[g] = (acc_sc[g] / l_sc[g]).astype(o_ref.dtype)


def attention(queries, kv_all, length, qbase, chunk):
    shards, _, width = kv_all.shape
    rows = queries.shape[1]
    tok = kv_all.shape[1] - chunk
    cache_parts = BLK // chunk
    new_parts = BLK // tok
    n_cache = shards // cache_parts
    n_new = shards // new_parts
    meta = jnp.stack([length, qbase]).astype(jnp.int32)
    kern = functools.partial(attn_kernel, n_cache=n_cache, rows=rows)
    return pl.pallas_call(
        kern,
        out_shape=jax.ShapeDtypeStruct((KVH, rows, HD), jnp.bfloat16),
        grid_spec=pltpu.PrefetchScalarGridSpec(
            num_scalar_prefetch=1,
            grid=(n_cache + n_new,),
            in_specs=[
                pl.BlockSpec((KVH, rows, HD), lambda i, m: (0, 0, 0)),
                pl.BlockSpec(
                    (cache_parts, chunk, width), lambda i, m: (jnp.minimum(i, n_cache - 1), 0, 0)
                ),
                pl.BlockSpec(
                    (new_parts, tok, width), lambda i, m: (jnp.maximum(i - n_cache, 0), chunk // tok, 0)
                ),
            ],
            out_specs=pl.BlockSpec((KVH, rows, HD), lambda i, m: (0, 0, 0)),
            scratch_shapes=[
                pltpu.VMEM((KVH, rows, 1), jnp.float32),
                pltpu.VMEM((KVH, rows, 1), jnp.float32),
                pltpu.VMEM((KVH, rows, HD), jnp.float32),
            ],
        ),
        compiler_params=pltpu.CompilerParams(dimension_semantics=("arbitrary",)),
    )(meta, queries, kv_all, kv_all)

def ffn_kernel(x_ref, w_ref, o_ref):
    rows = x_ref.shape[0] * x_ref.shape[2]
    x = x_ref[...].reshape(rows, D)
    w = w_ref[0]
    dims = (((1,), (1,)), ((), ()))
    gate = lax.dot_general(x, w[:, :D], dims, preferred_element_type=jnp.float32)
    upper = lax.dot_general(x, w[:, D : 2 * D], dims, preferred_element_type=jnp.float32)
    inner = (gate / (1.0 + jnp.exp(-gate)) * upper).astype(jnp.bfloat16)
    out = jnp.dot(inner, w[:, 2 * D :], preferred_element_type=jnp.float32)
    o_ref[...] = out.astype(o_ref.dtype).reshape(o_ref.shape)


def experts(arrived, weights):
    groups, count, capacity, _ = arrived.shape
    hidden = weights.shape[1]
    return pl.pallas_call(
        ffn_kernel,
        out_shape=jax.ShapeDtypeStruct(arrived.shape, jnp.bfloat16),
        grid=(count,),
        in_specs=[
            pl.BlockSpec((groups, 1, capacity, D), lambda j: (0, j, 0, 0)),
            pl.BlockSpec((1, hidden, 3 * D), lambda j: (j, 0, 0)),
        ],
        out_specs=pl.BlockSpec((groups, 1, capacity, D), lambda j: (0, j, 0, 0)),
        compiler_params=pltpu.CompilerParams(
            dimension_semantics=("arbitrary",), vmem_limit_bytes=48 * 1024 * 1024
        ),
    )(arrived, weights)


def rms_scale(values, gain):
    floats = values.astype(jnp.float32)
    inverse = lax.rsqrt(jnp.mean(floats * floats, axis=-1, keepdims=True) + EPSILON)
    return (floats * inverse * gain).astype(jnp.bfloat16)


def rotate(values, positions):
    half_dim = values.shape[-1] // 2
    freqs = jnp.power(10000.0, -jnp.arange(half_dim, dtype=jnp.float32) / half_dim)
    angles = positions.astype(jnp.float32)[:, None] * freqs[None, :]
    cosine = jnp.cos(angles)[:, None, :]
    sine = jnp.sin(angles)[:, None, :]
    first = values[..., :half_dim]
    second = values[..., half_dim:]
    return jnp.concatenate(
        [first * cosine - second * sine, second * cosine + first * sine], axis=-1
    )


def local(
    hidden_states,
    attn_gain,
    w_qkv,
    w_out,
    kv_cache,
    cached_len,
    ffn_gain,
    w_router,
    expert_ids,
    w_gate,
    w_up,
    w_down,
):
    groups = HEADS // KVH
    tok_rows = hidden_states.shape[0]
    shard_pos = lax.axis_index("shard")
    length = cached_len[0]
    normed = rms_scale(hidden_states, attn_gain)
    qkv = jnp.dot(normed, w_qkv, preferred_element_type=jnp.float32)
    positions = length + shard_pos * tok_rows + jnp.arange(tok_rows, dtype=jnp.int32)
    queries = rotate(qkv[:, : HEADS * HD].reshape(tok_rows, HEADS, HD), positions).astype(
        jnp.bfloat16
    )
    new_keys = rotate(
        qkv[:, HEADS * HD : (HEADS + KVH) * HD].reshape(tok_rows, KVH, HD), positions
    ).astype(jnp.bfloat16)
    new_values = qkv[:, (HEADS + KVH) * HD :].astype(jnp.bfloat16)
    new_kv = jnp.concatenate([new_keys.reshape(tok_rows, KVH * HD), new_values], axis=1)
    joined = jnp.concatenate([kv_cache[0], new_kv], axis=0)
    kv_all = lax.all_gather(joined, "shard", axis=0, tiled=False)
    query_rows = queries.reshape(tok_rows, KVH, groups, HD).transpose(1, 2, 0, 3)
    query_rows = query_rows.reshape(KVH, groups * tok_rows, HD)
    attended = attention(query_rows, kv_all, length, shard_pos * tok_rows, kv_cache.shape[1])
    attended = attended.reshape(KVH, groups, tok_rows, HD).transpose(2, 0, 1, 3)
    attended = attended.reshape(tok_rows, HEADS * HD)
    mid = (
        hidden_states.astype(jnp.float32)
        + jnp.dot(attended, w_out, preferred_element_type=jnp.float32)
    ).astype(jnp.bfloat16)
    normed2 = rms_scale(mid, ffn_gain)
    group_count = lax.axis_size("req")
    local_experts = w_gate.shape[0]
    expert_count = local_experts * group_count
    capacity = min(tok_rows, 5 * tok_rows * TOP // (4 * expert_count))
    logits = jnp.dot(normed2, w_router, preferred_element_type=jnp.float32)
    picked = expert_ids[:, :, None] == jnp.arange(expert_count, dtype=jnp.int32)[None, None, :]
    chosen = jnp.sum(jnp.where(picked, logits[:, None, :], 0.0), axis=-1)
    gates = jax.nn.softmax(chosen, axis=-1)
    flat_hot = picked.reshape(tok_rows * TOP, expert_count).astype(jnp.int32)
    ranks = jnp.cumsum(flat_hot, axis=0) - flat_hot
    slot_rank = jnp.sum(ranks * flat_hot, axis=-1)
    slots = expert_ids.reshape(-1) * capacity + slot_rank
    slot_table = (
        slots.reshape(tok_rows, TOP)[:, :, None]
        == jnp.arange(expert_count * capacity, dtype=jnp.int32)[None, None, :]
    )
    placing = jnp.any(slot_table, axis=1).astype(jnp.bfloat16)
    outgoing = jnp.einsum("ts,td->sd", placing, normed2, preferred_element_type=jnp.float32).astype(
        jnp.bfloat16
    )
    outgoing = outgoing.reshape(group_count, local_experts, capacity, D)
    arrived = lax.all_to_all(outgoing, "req", split_axis=0, concat_axis=0, tiled=True)
    token_of = jnp.repeat(jnp.arange(tok_rows, dtype=jnp.float32), TOP)
    tags = jnp.zeros((expert_count * capacity, 2), jnp.float32)
    tags = tags.at[:, 0].set(-1.0).at[slots].set(jnp.stack([token_of, gates.reshape(-1)], axis=-1))
    tags = tags.reshape(group_count, local_experts * capacity, 2)
    tags = lax.all_to_all(tags, "req", split_axis=0, concat_axis=0, tiled=True)
    weights = jnp.concatenate([w_gate, w_up, w_down], axis=-1)
    weights = lax.all_gather(weights, "shard", axis=1, tiled=True)
    expert_rows = experts(arrived, weights).astype(jnp.float32)
    expert_rows = expert_rows.reshape(group_count, local_experts * capacity, D)
    owner = tags[..., 0].astype(jnp.int32)
    weighting = jnp.where(
        owner[:, None, :] == jnp.arange(tok_rows, dtype=jnp.int32)[None, :, None], tags[:, None, :, 1], 0.0
    )
    partial = jnp.einsum(
        "stm,smd->std", weighting, expert_rows, preferred_element_type=jnp.float32,
        precision=lax.Precision.HIGH,
    )
    returned = lax.all_to_all(partial.astype(jnp.bfloat16), "req", split_axis=0, concat_axis=0, tiled=True)
    mixture = jnp.sum(returned.astype(jnp.float32), axis=0)
    return (mid.astype(jnp.float32) + mixture).astype(jnp.bfloat16)


def solution(mesh):
    return jax.shard_map(
        local,
        mesh=mesh,
        in_specs=(
            P(("req", "shard"), None),
            P(),
            P(),
            P(),
            P("req", "shard", None),
            P("req"),
            P(),
            P(),
            P(("req", "shard"), None),
            P("req", "shard", None),
            P("req", "shard", None),
            P("req", "shard", None),
        ),
        out_specs=P(("req", "shard"), None),
        check_vma=False,
    )
```

```python
import functools
import math

import jax
import jax.numpy as jnp
from jax import lax
from jax.experimental import pallas as pl
from jax.experimental.pallas import tpu as pltpu
from jax.sharding import PartitionSpec as P

D = 1536
HEADS = 24
KVH = 8
HD = 64
TOP = 8


EPSILON = 1e-05
NEG_FILL = -1e30
FAR_LIMIT = 1 << 30
BLK = 512
NEG = NEG_FILL

def attn_kernel(meta_ref, q_ref, cache_ref, new_ref, o_ref, m_sc, l_sc, acc_sc, *, n_cache, rows):
    i = pl.program_id(0)
    length = meta_ref[0]
    qbase = meta_ref[1]

    @pl.when(i == 0)
    def _():
        m_sc[...] = jnp.full(m_sc.shape, NEG, jnp.float32)
        l_sc[...] = jnp.zeros(l_sc.shape, jnp.float32)
        acc_sc[...] = jnp.zeros(acc_sc.shape, jnp.float32)

    def step(kv_ref, allowed):
        parts = kv_ref.shape[0]
        for g in range(KVH):
            q = q_ref[g]
            k = jnp.concatenate([kv_ref[c, :, g * HD:(g + 1) * HD] for c in range(parts)], axis=0)
            v = jnp.concatenate(
                [kv_ref[c, :, KVH * HD + g * HD:KVH * HD + (g + 1) * HD] for c in range(parts)], axis=0
            )
            s = lax.dot_general(q, k, (((1,), (1,)), ((), ())), preferred_element_type=jnp.float32) * (HD ** -0.5)
            s = jnp.where(allowed, s, NEG)
            m_prev = m_sc[g]
            m_new = jnp.maximum(m_prev, jnp.max(s, axis=-1, keepdims=True))
            p = jnp.where(allowed, jnp.exp(s - m_new), 0.0)
            factor = jnp.exp(m_prev - m_new)
            l_sc[g] = l_sc[g] * factor + jnp.sum(p, axis=-1, keepdims=True)
            acc_sc[g] = acc_sc[g] * factor + jnp.dot(p.astype(jnp.bfloat16), v, preferred_element_type=jnp.float32)
            m_sc[g] = m_new

    @pl.when((i < n_cache) & (i * BLK < length))
    def _():
        key = i * BLK + lax.broadcasted_iota(jnp.int32, (rows, BLK), 1)
        step(cache_ref, key < length)

    j = i - n_cache
    tok = rows // (HEADS // KVH)

    @pl.when((i >= n_cache) & (j * BLK <= qbase + tok - 1))
    def _():
        key = j * BLK + lax.broadcasted_iota(jnp.int32, (rows, BLK), 1)
        qpos = qbase + lax.broadcasted_iota(jnp.int32, (rows, BLK), 0) % tok
        step(new_ref, key <= qpos)

    @pl.when(i == pl.num_programs(0) - 1)
    def _():
        for g in range(KVH):
            o_ref[g] = (acc_sc[g] / l_sc[g]).astype(o_ref.dtype)


def attention(queries, kv_all, length, qbase, chunk):
    shards, _, width = kv_all.shape
    rows = queries.shape[1]
    tok = kv_all.shape[1] - chunk
    cache_parts = BLK // chunk
    new_parts = BLK // tok
    n_cache = shards // cache_parts
    n_new = shards // new_parts
    meta = jnp.stack([length, qbase]).astype(jnp.int32)
    kern = functools.partial(attn_kernel, n_cache=n_cache, rows=rows)
    return pl.pallas_call(
        kern,
        out_shape=jax.ShapeDtypeStruct((KVH, rows, HD), jnp.bfloat16),
        grid_spec=pltpu.PrefetchScalarGridSpec(
            num_scalar_prefetch=1,
            grid=(n_cache + n_new,),
            in_specs=[
                pl.BlockSpec((KVH, rows, HD), lambda i, m: (0, 0, 0)),
                pl.BlockSpec(
                    (cache_parts, chunk, width), lambda i, m: (jnp.minimum(i, n_cache - 1), 0, 0)
                ),
                pl.BlockSpec(
                    (new_parts, tok, width), lambda i, m: (jnp.maximum(i - n_cache, 0), chunk // tok, 0)
                ),
            ],
            out_specs=pl.BlockSpec((KVH, rows, HD), lambda i, m: (0, 0, 0)),
            scratch_shapes=[
                pltpu.VMEM((KVH, rows, 1), jnp.float32),
                pltpu.VMEM((KVH, rows, 1), jnp.float32),
                pltpu.VMEM((KVH, rows, HD), jnp.float32),
            ],
        ),
        compiler_params=pltpu.CompilerParams(dimension_semantics=("arbitrary",)),
    )(meta, queries, kv_all, kv_all)

def ffn_kernel(x_ref, w_ref, o_ref):
    rows = x_ref.shape[0] * x_ref.shape[2]
    x = x_ref[...].reshape(rows, D)
    w = w_ref[0]
    dims = (((1,), (1,)), ((), ()))
    gate = lax.dot_general(x, w[:, :D], dims, preferred_element_type=jnp.float32)
    upper = lax.dot_general(x, w[:, D : 2 * D], dims, preferred_element_type=jnp.float32)
    inner = (gate / (1.0 + jnp.exp(-gate)) * upper).astype(jnp.bfloat16)
    out = jnp.dot(inner, w[:, 2 * D :], preferred_element_type=jnp.float32)
    o_ref[...] = out.astype(o_ref.dtype).reshape(o_ref.shape)


def experts(arrived, weights):
    groups, count, capacity, _ = arrived.shape
    hidden = weights.shape[1]
    return pl.pallas_call(
        ffn_kernel,
        out_shape=jax.ShapeDtypeStruct(arrived.shape, jnp.bfloat16),
        grid=(count,),
        in_specs=[
            pl.BlockSpec((groups, 1, capacity, D), lambda j: (0, j, 0, 0)),
            pl.BlockSpec((1, hidden, 3 * D), lambda j: (j, 0, 0)),
        ],
        out_specs=pl.BlockSpec((groups, 1, capacity, D), lambda j: (0, j, 0, 0)),
        compiler_params=pltpu.CompilerParams(
            dimension_semantics=("arbitrary",), vmem_limit_bytes=48 * 1024 * 1024
        ),
    )(arrived, weights)


def rms_scale(values, gain):
    floats = values.astype(jnp.float32)
    inverse = lax.rsqrt(jnp.mean(floats * floats, axis=-1, keepdims=True) + EPSILON)
    return (floats * inverse * gain).astype(jnp.bfloat16)


def rotate(values, positions):
    half_dim = values.shape[-1] // 2
    freqs = jnp.power(10000.0, -jnp.arange(half_dim, dtype=jnp.float32) / half_dim)
    angles = positions.astype(jnp.float32)[:, None] * freqs[None, :]
    cosine = jnp.cos(angles)[:, None, :]
    sine = jnp.sin(angles)[:, None, :]
    first = values[..., :half_dim]
    second = values[..., half_dim:]
    return jnp.concatenate(
        [first * cosine - second * sine, second * cosine + first * sine], axis=-1
    )


def local(
    hidden_states,
    attn_gain,
    w_qkv,
    w_out,
    kv_cache,
    cached_len,
    ffn_gain,
    w_router,
    expert_ids,
    w_gate,
    w_up,
    w_down,
):
    groups = HEADS // KVH
    tok_rows = hidden_states.shape[0]
    shard_pos = lax.axis_index("shard")
    length = cached_len[0]
    normed = rms_scale(hidden_states, attn_gain)
    qkv = jnp.dot(normed, w_qkv, preferred_element_type=jnp.float32)
    positions = length + shard_pos * tok_rows + jnp.arange(tok_rows, dtype=jnp.int32)
    queries = rotate(qkv[:, : HEADS * HD].reshape(tok_rows, HEADS, HD), positions).astype(
        jnp.bfloat16
    )
    new_keys = rotate(
        qkv[:, HEADS * HD : (HEADS + KVH) * HD].reshape(tok_rows, KVH, HD), positions
    ).astype(jnp.bfloat16)
    new_values = qkv[:, (HEADS + KVH) * HD :].astype(jnp.bfloat16)
    new_kv = jnp.concatenate([new_keys.reshape(tok_rows, KVH * HD), new_values], axis=1)
    joined = jnp.concatenate([kv_cache[0], new_kv], axis=0)
    kv_all = lax.all_gather(joined, "shard", axis=0, tiled=False)
    query_rows = queries.reshape(tok_rows, KVH, groups, HD).transpose(1, 2, 0, 3)
    query_rows = query_rows.reshape(KVH, groups * tok_rows, HD)
    attended = attention(query_rows, kv_all, length, shard_pos * tok_rows, kv_cache.shape[1])
    attended = attended.reshape(KVH, groups, tok_rows, HD).transpose(2, 0, 1, 3)
    attended = attended.reshape(tok_rows, HEADS * HD)
    mid = (
        hidden_states.astype(jnp.float32)
        + jnp.dot(attended, w_out, preferred_element_type=jnp.float32)
    ).astype(jnp.bfloat16)
    normed2 = rms_scale(mid, ffn_gain)
    group_count = lax.axis_size("req")
    local_experts = w_gate.shape[0]
    expert_count = local_experts * group_count
    capacity = min(tok_rows, 5 * tok_rows * TOP // (4 * expert_count))
    logits = jnp.dot(normed2, w_router, preferred_element_type=jnp.float32)
    picked = expert_ids[:, :, None] == jnp.arange(expert_count, dtype=jnp.int32)[None, None, :]
    chosen = jnp.sum(jnp.where(picked, logits[:, None, :], 0.0), axis=-1)
    gates = jax.nn.softmax(chosen, axis=-1)
    flat_hot = picked.reshape(tok_rows * TOP, expert_count).astype(jnp.int32)
    pairs = flat_hot.shape[0]
    before = (
        lax.broadcasted_iota(jnp.int32, (pairs, pairs), 1)
        < lax.broadcasted_iota(jnp.int32, (pairs, pairs), 0) + 0 * shard_pos
    ).astype(jnp.bfloat16)
    ranks = jnp.dot(before, flat_hot.astype(jnp.bfloat16), preferred_element_type=jnp.float32)
    ranks = ranks.astype(jnp.int32)
    slot_rank = jnp.sum(ranks * flat_hot, axis=-1)
    slots = expert_ids.reshape(-1) * capacity + slot_rank
    slot_table = (
        slots.reshape(tok_rows, TOP)[:, :, None]
        == jnp.arange(expert_count * capacity, dtype=jnp.int32)[None, None, :]
    )
    placing = jnp.any(slot_table, axis=1).astype(jnp.bfloat16)
    outgoing = jnp.einsum("ts,td->sd", placing, normed2, preferred_element_type=jnp.float32).astype(
        jnp.bfloat16
    )
    outgoing = outgoing.reshape(group_count, local_experts, capacity, D)
    arrived = lax.all_to_all(outgoing, "req", split_axis=0, concat_axis=0, tiled=True)
    token_of = jnp.repeat(jnp.arange(tok_rows, dtype=jnp.float32), TOP)
    tags = jnp.zeros((expert_count * capacity, 2), jnp.float32)
    tags = tags.at[:, 0].set(-1.0).at[slots].set(jnp.stack([token_of, gates.reshape(-1)], axis=-1))
    tags = tags.reshape(group_count, local_experts * capacity, 2)
    tags = lax.all_to_all(tags, "req", split_axis=0, concat_axis=0, tiled=True)
    weights = jnp.concatenate([w_gate, w_up, w_down], axis=-1)
    weights = lax.all_gather(weights, "shard", axis=1, tiled=True)
    expert_rows = experts(arrived, weights).astype(jnp.float32)
    expert_rows = expert_rows.reshape(group_count, local_experts * capacity, D)
    owner = tags[..., 0].astype(jnp.int32)
    weighting = jnp.where(
        owner[:, None, :] == jnp.arange(tok_rows, dtype=jnp.int32)[None, :, None], tags[:, None, :, 1], 0.0
    )
    partial = jnp.einsum(
        "stm,smd->std", weighting, expert_rows, preferred_element_type=jnp.float32,
        precision=lax.Precision.HIGHEST,
    )
    returned = lax.all_to_all(partial.astype(jnp.bfloat16), "req", split_axis=0, concat_axis=0, tiled=True)
    mixture = jnp.sum(returned.astype(jnp.float32), axis=0)
    return (mid.astype(jnp.float32) + mixture).astype(jnp.bfloat16)


def solution(mesh):
    return jax.shard_map(
        local,
        mesh=mesh,
        in_specs=(
            P(("req", "shard"), None),
            P(),
            P(),
            P(),
            P("req", "shard", None),
            P("req"),
            P(),
            P(),
            P(("req", "shard"), None),
            P("req", "shard", None),
            P("req", "shard", None),
            P("req", "shard", None),
        ),
        out_specs=P(("req", "shard"), None),
        check_vma=False,
    )
```
